512 devices in a mesh: tile: 128 (over z, y_hi, x), lev: 4 (over y_lo, core).
Axes of the slice: x: 4, y: 4 (y_hi: 2, y_lo: 2; y = y_hi * 2 + y_lo), z: 16, core: 2. Of those that a mesh axis runs over, the one named last changes fastest.
Arguments:
- forcing: float32 [2, 52, 6144, 128], P(None, 'lev', 'tile'), may hold values from -6 to 6
- lateral_mix: float32 [52], P('lev'), may hold values from 0.05 to 0.15
- sea_mask: int32 [6144, 128], P('tile'), may hold values 0 or 1
- convective: int32 [6144, 128], P('tile'), may hold values 0 or 1
- mixing_inverse: float32 [2, 2, 52, 52], replicated, may hold values from -1.5 to 1.5
- seam_links: int32 [128, 8], P('tile'), may hold values from 0 to 511, as said below
Outputs:
- swept: float32 [2, 52, 6144, 128], P(None, 'lev', 'tile')
The draws below stay inside these ranges and needn't reach their ends.
Inputs may be any that keep to these rules, and one draw needn't show every extreme that they name: Tile t sits at row t // 16 and column t % (16) of a grid of 8 rows that closes in both directions. seam_links[t, k] = 4 * s + code, where s is the tile beside t in that grid toward the previous row (k = 0), the next row (k = 1), the previous column (k = 2), the next column (k = 3), and diagonally (k = 4: previous row and column, 5: previous row and next column, 6: next row and previous column, 7: next row and next column).
All inputs are finite; a program needn't handle non-finite values. No bound on the sum of `sea_mask` or of `convective` on one device may be relied on, other than what follows from the above.
Results may differ from the reference program's by a relative error of at most 0.0001.
Values sent between devices are 32-bit elements; how exact they have to be, the bound alone decides.
No kernel may reach another device: no remote copies, remote signals or barrier semaphores. Data moves between devices by JAX's collectives and lax.ppermute only.
A program may use at most 64 MiB of HBM per device.

```python
import math
import jax
import jax.numpy as jnp
from jax import lax

LEV = 52
CX = 48
CY = 128
STEPS = 2
ROWS = 6144
N_TILE = 128


def draw_seam_links(key, part):
    tile_ids = jnp.arange(N_TILE, dtype=jnp.int32)
    width = N_TILE // 8
    grid_row = tile_ids // width
    grid_col = tile_ids % width
    row_step = jnp.array([-1, 1, 0, 0, -1, -1, 1, 1], jnp.int32)
    col_step = jnp.array([0, 0, -1, 1, -1, 1, -1, 1], jnp.int32)
    source = (grid_row[:, None] + row_step[None, :]) % 8 * width + (grid_col[:, None] + col_step[None, :]) % width
    codes = jax.random.randint(key, (N_TILE, 8), 0, 4, dtype=jnp.int32)
    return (source * 4 + codes).astype(jnp.int32)


def draw_mixing_inverse(key, part):
    key_off = jax.random.fold_in(key, 11)
    key_diag = jax.random.fold_in(key, 23)
    spread = jnp.clip(jax.random.normal(key_off, (2, 2, LEV, LEV), jnp.float32), -4.0, 4.0)
    scale = jnp.array([0.6, 1.2], jnp.float32)[None, :, None, None] / jnp.sqrt(jnp.float32(LEV))
    diagonal = 1.0 + 0.5 * jax.random.uniform(key_diag, (2, 2, LEV), jnp.float32)
    unit = jnp.eye(LEV, dtype=jnp.float32)
    return (spread * scale * (1.0 - unit) + unit * diagonal[..., None]).astype(jnp.float32)


def set_ends(entries, stream_key, least, top_value):
    index_at = [jax.random.randint(jax.random.fold_in(stream_key, axis), (), 0, length) for axis, length in enumerate(entries.shape)]
    longest = entries.shape.index(max(entries.shape))
    next_to = index_at[:longest] + [(index_at[longest] + 1) % entries.shape[longest]] + index_at[longest + 1:]
    return entries.at[tuple(index_at)].set(least).at[tuple(next_to)].set(top_value)


def level_of(rng, shape, shards, least, top_value):
    factor_of, own = 1.0, jax.random.fold_in(rng, 6)
    for position, parts in shards:
        steps = jnp.exp(jax.random.uniform(jax.random.fold_in(own, position), (parts,), jnp.float32, least / len(shards), top_value / len(shards)))
        factor_of = factor_of * jnp.repeat(steps, shape[position] // parts).reshape([-1 if axis == position else 1 for axis in range(len(shape))])
    return factor_of


def gaussian(own_key, extent, scale, limit, shards=(), kind=jnp.bfloat16):
    values = scale * jax.random.normal(own_key, extent, jnp.float32)
    if shards:
        values = values * level_of(own_key, extent, shards, -0.22, 0.18)
    return jnp.clip(values, -limit, limit).astype(kind)


def setup_inputs(seed: int = 0) -> dict:
    arg_keys = jax.random.split(jax.random.key(seed), 7)
    forcing = gaussian(arg_keys[0], (2, LEV, ROWS, CY), 1.0, 6.0, ((1, 4), (2, 128)), jnp.float32)
    lateral_mix = jnp.clip(jnp.exp(math.log(0.15) - 1.0986123 * jax.random.uniform(arg_keys[1], (LEV,), jnp.float32) ** level_of(arg_keys[1], (LEV,), ((0, 4),), -0.2, 0.2)), 0.05, 0.15)
    sea_mask = set_ends((jax.random.randint(arg_keys[2], (ROWS, CY), 0, 5) < 4).astype(jnp.int32), jax.random.fold_in(arg_keys[2], 1), 0, 1)
    convective = set_ends((jax.random.randint(arg_keys[3], (ROWS, CY), 0, 3) < 1).astype(jnp.int32), jax.random.fold_in(arg_keys[3], 1), 0, 1)
    mixing_inverse = draw_mixing_inverse(jax.random.fold_in(arg_keys[6], 71), 0)
    seam_links = draw_seam_links(jax.random.fold_in(arg_keys[6], 71), 0)
    return {"forcing": forcing, "lateral_mix": lateral_mix, "sea_mask": sea_mask, "convective": convective, "mixing_inverse": mixing_inverse, "seam_links": seam_links}


def strip_set(field):
    return jnp.concatenate([field[..., 0, :], field[..., -1, :], field[..., :, 0], field[..., :, -1], field[..., 0, 0:1], field[..., 0, -1:], field[..., -1, 0:1], field[..., -1, -1:]], axis=-1)


def assemble(field, south, north, west, east, corners):
    middle = jnp.concatenate([west[..., None], field, east[..., None]], axis=-1)
    top_row = jnp.concatenate([corners[0][..., None], south, corners[1][..., None]], axis=-1)
    bottom_row = jnp.concatenate([corners[2][..., None], north, corners[3][..., None]], axis=-1)
    return jnp.concatenate([top_row[..., None, :], middle, bottom_row[..., None, :]], axis=-2)


def stencil(extended, field, rate, wet):
    edge_sum = ((extended[..., :-2, 1:-1] + extended[..., 2:, 1:-1]) + extended[..., 1:-1, :-2]) + extended[..., 1:-1, 2:]
    diag_sum = ((extended[..., :-2, :-2] + extended[..., :-2, 2:]) + extended[..., 2:, :-2]) + extended[..., 2:, 2:]
    return wet * ((1.0 - 6.0 * rate) * field + rate * edge_sum + 0.5 * rate * diag_sum)


def horizontal(adjoint, lateral_mix, wet, seam_links):
    tiles = adjoint.reshape(2, LEV, N_TILE, CX, CY)
    strips = strip_set(tiles)
    source = (seam_links // 4).astype(jnp.int32)
    codes = (seam_links % 4).astype(jnp.int32)
    chosen = jnp.take(strips, source, axis=2)

    def edge(slot, first, last, length):
        code = codes[:, slot][None, None, :, None]
        part_a = chosen[:, :, :, slot, first:first + length]
        part_b = chosen[:, :, :, slot, last:last + length]
        strip = jnp.where(code % 2 == 0, part_a, part_b)
        return jnp.where(code // 2 == 1, strip[..., ::-1], strip)

    base = 2 * CY + 2 * CX

    def corner(slot):
        index = (base + codes[:, slot]).astype(jnp.int32)
        return jnp.take_along_axis(chosen[:, :, :, slot, :], index[None, None, :, None], axis=3)[..., 0]

    south = edge(0, 0, CY, CY)
    north = edge(1, 0, CY, CY)
    west = edge(2, 2 * CY, 2 * CY + CX, CX)
    east = edge(3, 2 * CY, 2 * CY + CX, CX)
    corners = [corner(4), corner(5), corner(6), corner(7)]
    extended = assemble(tiles, south, north, west, east, corners)
    rate = lateral_mix[None, :, None, None, None]
    result = stencil(extended, tiles, rate, wet[None, None])
    return result.reshape(2, LEV, N_TILE * CX, CY)


def reference(forcing, lateral_mix, sea_mask, convective, mixing_inverse, seam_links):
    wet = sea_mask.astype(jnp.float32).reshape(N_TILE, CX, CY)
    adjoint = forcing
    for step in range(STEPS):
        lateral = horizontal(adjoint, lateral_mix, wet, seam_links)
        plain = jnp.einsum('tml,tmxy->tlxy', mixing_inverse[:, 0], lateral, precision=lax.Precision.HIGHEST)
        mixed = jnp.einsum('tml,tmxy->tlxy', mixing_inverse[:, 1], lateral, precision=lax.Precision.HIGHEST)
        adjoint = jnp.where(convective[None, None] == 1, mixed, plain)
    return adjoint
```

```python
import jax
import jax.numpy as jnp
from jax import lax
from jax.sharding import PartitionSpec as P

STEPS = 2
GRID_ROWS = 8

SLOT_STEPS = ((-1, 0), (1, 0), (0, -1), (0, 1), (-1, -1), (-1, 1), (1, -1), (1, 1))


def slot_pairs(count, slot):
    width = count // GRID_ROWS
    row_move, col_move = SLOT_STEPS[slot]
    pairs = []
    for target in range(count):
        row, col = divmod(target, width)
        source = ((row + row_move) % GRID_ROWS) * width + (col + col_move) % width
        pairs.append((source, target))
    return pairs


def pick(pair, code):
    strip = jnp.where(code % 2 == 0, pair[..., 0, :], pair[..., 1, :])
    return jnp.where(code // 2 == 1, strip[..., ::-1], strip)


def stencil(extended, field, rate, wet):
    edge_sum = (
        extended[..., :-2, 1:-1]
        + extended[..., 2:, 1:-1]
        + extended[..., 1:-1, :-2]
        + extended[..., 1:-1, 2:]
    )
    diag_sum = (
        extended[..., :-2, :-2]
        + extended[..., :-2, 2:]
        + extended[..., 2:, :-2]
        + extended[..., 2:, 2:]
    )
    return wet * ((1.0 - 6.0 * rate) * field + rate * edge_sum + 0.5 * rate * diag_sum)


def horizontal(field, rate, wet, codes):
    count = lax.axis_size("tile")
    row_pair = jnp.stack([field[..., 0, :], field[..., -1, :]], axis=-2)
    col_pair = jnp.stack([field[..., :, 0], field[..., :, -1]], axis=-2)
    corner_set = jnp.stack(
        [field[..., 0, 0], field[..., 0, -1], field[..., -1, 0], field[..., -1, -1]], axis=-1
    )
    payloads = [row_pair, row_pair, col_pair, col_pair] + [corner_set] * 4
    got = [lax.ppermute(payloads[slot], "tile", slot_pairs(count, slot)) for slot in range(8)]
    south = pick(got[0], codes[0])
    north = pick(got[1], codes[1])
    west = pick(got[2], codes[2])
    east = pick(got[3], codes[3])
    corners = []
    for slot in range(4, 8):
        cell = got[slot]
        code = codes[slot]
        value = jnp.where(
            code == 0,
            cell[..., 0],
            jnp.where(code == 1, cell[..., 1], jnp.where(code == 2, cell[..., 2], cell[..., 3])),
        )
        corners.append(value)
    middle = jnp.concatenate([west[..., None], field, east[..., None]], axis=-1)
    top_row = jnp.concatenate([corners[0][..., None], south, corners[1][..., None]], axis=-1)
    bottom_row = jnp.concatenate([corners[2][..., None], north, corners[3][..., None]], axis=-1)
    extended = jnp.concatenate([top_row[..., None, :], middle, bottom_row[..., None, :]], axis=-2)
    return stencil(extended, field, rate, wet)


def column_mix(lateral, mixing_inverse, convective_rows):
    columns = lax.all_to_all(lateral, "lev", 2, 1, tiled=True)
    both_states = jnp.einsum(
        "tsml,tmxy->tslxy", mixing_inverse, columns, precision=lax.Precision.HIGHEST
    )
    mixed = jnp.where(convective_rows[None, None], both_states[:, 1], both_states[:, 0])
    return lax.all_to_all(mixed, "lev", 1, 2, tiled=True)


def local(forcing, lateral_mix, sea_mask, convective, mixing_inverse, seam_links):
    wet = sea_mask.astype(jnp.float32)[None, None]
    rate = lateral_mix[None, :, None, None]
    codes = seam_links[0] % 4
    parts = lax.axis_size("lev")
    rows = forcing.shape[2] // parts
    lev_here = lax.axis_index("lev")
    convective_rows = lax.dynamic_slice_in_dim(convective, lev_here * rows, rows, axis=0) == 1
    adjoint = forcing
    for step in range(STEPS):
        lateral = horizontal(adjoint, rate, wet, codes)
        adjoint = column_mix(lateral, mixing_inverse, convective_rows)
    return adjoint


def solution(mesh):
    return jax.shard_map(
        local,
        mesh=mesh,
        in_specs=(
            P(None, "lev", "tile", None),
            P("lev"),
            P("tile", None),
            P("tile", None),
            P(),
            P("tile", None),
        ),
        out_specs=P(None, "lev", "tile", None),
        check_vma=False,
    )
```

```python
import jax
import jax.numpy as jnp
from jax import lax
from jax.sharding import PartitionSpec as P

STEPS = 2
GRID_ROWS = 8

SLOT_STEPS = ((-1, 0), (1, 0), (0, -1), (0, 1), (-1, -1), (-1, 1), (1, -1), (1, 1))


def slot_pairs(count, slot):
    width = count // GRID_ROWS
    row_move, col_move = SLOT_STEPS[slot]
    pairs = []
    for target in range(count):
        row, col = divmod(target, width)
        source = ((row + row_move) % GRID_ROWS) * width + (col + col_move) % width
        pairs.append((source, target))
    return pairs


def pick(pair, code):
    strip = jnp.where(code % 2 == 0, pair[..., 0, :], pair[..., 1, :])
    return jnp.where(code // 2 == 1, strip[..., ::-1], strip)


def stencil(extended, field, rate, wet):
    edge_sum = (
        extended[..., :-2, 1:-1]
        + extended[..., 2:, 1:-1]
        + extended[..., 1:-1, :-2]
        + extended[..., 1:-1, 2:]
    )
    diag_sum = (
        extended[..., :-2, :-2]
        + extended[..., :-2, 2:]
        + extended[..., 2:, :-2]
        + extended[..., 2:, 2:]
    )
    return wet * ((1.0 - 6.0 * rate) * field + rate * edge_sum + 0.5 * rate * diag_sum)


def horizontal(field, rate, wet, codes):
    count = lax.axis_size("tile")
    corner_set = jnp.stack(
        [field[..., 0, 0], field[..., 0, -1], field[..., -1, 0], field[..., -1, -1]], axis=-1
    )
    side = jnp.concatenate([field[..., :, 0], field[..., :, -1], corner_set], axis=-1)
    from_west = lax.ppermute(side, "tile", slot_pairs(count, 2))
    from_east = lax.ppermute(side, "tile", slot_pairs(count, 3))
    cols = field.shape[-1]
    rows = field.shape[-2]
    span = 2 * rows
    upright = jnp.concatenate(
        [field[..., 0, :], field[..., -1, :], from_west[..., span:], from_east[..., span:]], axis=-1
    )
    from_south = lax.ppermute(upright, "tile", slot_pairs(count, 0))
    from_north = lax.ppermute(upright, "tile", slot_pairs(count, 1))

    def strips(got, length):
        return jnp.stack([got[..., :length], got[..., length : 2 * length]], axis=-2)

    south = pick(strips(from_south, cols), codes[0])
    north = pick(strips(from_north, cols), codes[1])
    west = pick(strips(from_west, rows), codes[2])
    east = pick(strips(from_east, rows), codes[3])
    base = 2 * cols
    sources = [
        (from_south, base),
        (from_south, base + 4),
        (from_north, base),
        (from_north, base + 4),
    ]
    corners = []
    for slot, (got, first) in zip(range(4, 8), sources):
        code = codes[slot]
        cell = got[..., first : first + 4]
        value = jnp.where(
            code == 0,
            cell[..., 0],
            jnp.where(code == 1, cell[..., 1], jnp.where(code == 2, cell[..., 2], cell[..., 3])),
        )
        corners.append(value)
    middle = jnp.concatenate([west[..., None], field, east[..., None]], axis=-1)
    top_row = jnp.concatenate([corners[0][..., None], south, corners[1][..., None]], axis=-1)
    bottom_row = jnp.concatenate([corners[2][..., None], north, corners[3][..., None]], axis=-1)
    extended = jnp.concatenate([top_row[..., None, :], middle, bottom_row[..., None, :]], axis=-2)
    return stencil(extended, field, rate, wet)


def column_mix(lateral, mixing_inverse, convective_rows):
    columns = lax.all_to_all(lateral, "lev", 2, 1, tiled=True)
    both_states = jnp.einsum(
        "tsml,tmxy->tslxy", mixing_inverse, columns, precision=lax.Precision.HIGHEST
    )
    mixed = jnp.where(convective_rows[None, None], both_states[:, 1], both_states[:, 0])
    return lax.all_to_all(mixed, "lev", 1, 2, tiled=True)


def local(forcing, lateral_mix, sea_mask, convective, mixing_inverse, seam_links):
    wet = sea_mask.astype(jnp.float32)[None, None]
    rate = lateral_mix[None, :, None, None]
    codes = seam_links[0] % 4
    parts = lax.axis_size("lev")
    rows = forcing.shape[2] // parts
    lev_here = lax.axis_index("lev")
    convective_rows = lax.dynamic_slice_in_dim(convective, lev_here * rows, rows, axis=0) == 1
    adjoint = forcing
    for step in range(STEPS):
        lateral = horizontal(adjoint, rate, wet, codes)
        adjoint = column_mix(lateral, mixing_inverse, convective_rows)
    return adjoint


def solution(mesh):
    return jax.shard_map(
        local,
        mesh=mesh,
        in_specs=(
            P(None, "lev", "tile", None),
            P("lev"),
            P("tile", None),
            P("tile", None),
            P(),
            P("tile", None),
        ),
        out_specs=P(None, "lev", "tile", None),
        check_vma=False,
    )
```

```python
import jax
import jax.numpy as jnp
from jax import lax
from jax.sharding import PartitionSpec as P

STEPS = 2
GRID_ROWS = 8

SLOT_STEPS = ((-1, 0), (1, 0), (0, -1), (0, 1), (-1, -1), (-1, 1), (1, -1), (1, 1))


def slot_pairs(count, slot):
    width = count // GRID_ROWS
    row_move, col_move = SLOT_STEPS[slot]
    pairs = []
    for target in range(count):
        row, col = divmod(target, width)
        source = ((row + row_move) % GRID_ROWS) * width + (col + col_move) % width
        pairs.append((source, target))
    return pairs


def pick(pair, code):
    strip = jnp.where(code % 2 == 0, pair[..., 0, :], pair[..., 1, :])
    return jnp.where(code // 2 == 1, strip[..., ::-1], strip)


def stencil(extended, field, rate, wet):
    edge_sum = (
        extended[..., :-2, 1:-1]
        + extended[..., 2:, 1:-1]
        + extended[..., 1:-1, :-2]
        + extended[..., 1:-1, 2:]
    )
    diag_sum = (
        extended[..., :-2, :-2]
        + extended[..., :-2, 2:]
        + extended[..., 2:, :-2]
        + extended[..., 2:, 2:]
    )
    return wet * ((1.0 - 6.0 * rate) * field + rate * edge_sum + 0.5 * rate * diag_sum)


def horizontal(field, rate, wet, codes):
    count = lax.axis_size("tile")
    corner_set = jnp.stack(
        [field[..., 0, 0], field[..., 0, -1], field[..., -1, 0], field[..., -1, -1]], axis=-1
    )
    side = jnp.concatenate([field[..., :, 0], field[..., :, -1], corner_set], axis=-1)
    from_west = lax.ppermute(side, "tile", slot_pairs(count, 2))
    from_east = lax.ppermute(side, "tile", slot_pairs(count, 3))
    cols = field.shape[-1]
    rows = field.shape[-2]
    span = 2 * rows
    upright = jnp.concatenate(
        [field[..., 0, :], field[..., -1, :], from_west[..., span:], from_east[..., span:]], axis=-1
    )
    from_south = lax.ppermute(upright, "tile", slot_pairs(count, 0))
    from_north = lax.ppermute(upright, "tile", slot_pairs(count, 1))

    def strips(got, length):
        return jnp.stack([got[..., :length], got[..., length : 2 * length]], axis=-2)

    south = pick(strips(from_south, cols), codes[0])
    north = pick(strips(from_north, cols), codes[1])
    west = pick(strips(from_west, rows), codes[2])
    east = pick(strips(from_east, rows), codes[3])
    base = 2 * cols
    sources = [
        (from_south, base),
        (from_south, base + 4),
        (from_north, base),
        (from_north, base + 4),
    ]
    corners = []
    for slot, (got, first) in zip(range(4, 8), sources):
        code = codes[slot]
        cell = got[..., first : first + 4]
        value = jnp.where(
            code == 0,
            cell[..., 0],
            jnp.where(code == 1, cell[..., 1], jnp.where(code == 2, cell[..., 2], cell[..., 3])),
        )
        corners.append(value)
    middle = jnp.concatenate([west[..., None], field, east[..., None]], axis=-1)
    top_row = jnp.concatenate([corners[0][..., None], south, corners[1][..., None]], axis=-1)
    bottom_row = jnp.concatenate([corners[2][..., None], north, corners[3][..., None]], axis=-1)
    extended = jnp.concatenate([top_row[..., None, :], middle, bottom_row[..., None, :]], axis=-2)
    return stencil(extended, field, rate, wet)


def column_mix(lateral, stacked_inverse, convective_rows):
    parts = lax.axis_size("lev")
    tracers, depth, rows, cols = lateral.shape
    part_rows = rows // parts
    outgoing = jnp.transpose(
        lateral.reshape(tracers, depth, parts, part_rows, cols), (2, 0, 1, 3, 4)
    )
    columns = lax.all_to_all(outgoing, "lev", 0, 0, tiled=True)
    mixed = []
    for tracer in range(tracers):
        flat = columns[:, tracer].reshape(parts * depth, part_rows * cols)
        both_states = jnp.dot(
            stacked_inverse[tracer], flat, precision=lax.Precision.HIGHEST
        ).reshape(2, parts, depth, part_rows, cols)
        mixed.append(jnp.where(convective_rows[None, None], both_states[1], both_states[0]))
    returning = lax.all_to_all(jnp.stack(mixed, axis=1), "lev", 0, 0, tiled=True)
    return jnp.transpose(returning, (1, 2, 0, 3, 4)).reshape(tracers, depth, rows, cols)


def local(forcing, lateral_mix, sea_mask, convective, mixing_inverse, seam_links):
    wet = sea_mask.astype(jnp.float32)[None]
    plane_rate = jnp.tile(lateral_mix, forcing.shape[0])[:, None, None]
    codes = seam_links[0] % 4
    parts = lax.axis_size("lev")
    rows = forcing.shape[2] // parts
    lev_here = lax.axis_index("lev")
    convective_rows = lax.dynamic_slice_in_dim(convective, lev_here * rows, rows, axis=0) == 1
    stacked_inverse = jnp.swapaxes(mixing_inverse, 2, 3).reshape(
        mixing_inverse.shape[0], -1, mixing_inverse.shape[2]
    )
    tracers, depth, rows, cols = forcing.shape
    adjoint = forcing
    for step in range(STEPS):
        planes = adjoint.reshape(tracers * depth, rows, cols)
        lateral = horizontal(planes, plane_rate, wet, codes)
        adjoint = column_mix(lateral.reshape(tracers, depth, rows, cols), stacked_inverse, convective_rows)
    return adjoint


def solution(mesh):
    return jax.shard_map(
        local,
        mesh=mesh,
        in_specs=(
            P(None, "lev", "tile", None),
            P("lev"),
            P("tile", None),
            P("tile", None),
            P(),
            P("tile", None),
        ),
        out_specs=P(None, "lev", "tile", None),
        check_vma=False,
    )
```

```python
import jax
import jax.numpy as jnp
from jax import lax
from jax.sharding import PartitionSpec as P

STEPS = 2
GRID_ROWS = 8

SLOT_STEPS = ((-1, 0), (1, 0), (0, -1), (0, 1), (-1, -1), (-1, 1), (1, -1), (1, 1))


def slot_pairs(count, slot):
    width = count // GRID_ROWS
    row_move, col_move = SLOT_STEPS[slot]
    pairs = []
    for target in range(count):
        row, col = divmod(target, width)
        source = ((row + row_move) % GRID_ROWS) * width + (col + col_move) % width
        pairs.append((source, target))
    return pairs


def pick(pair, code):
    strip = jnp.where(code % 2 == 0, pair[..., 0, :], pair[..., 1, :])
    return jnp.where(code // 2 == 1, strip[..., ::-1], strip)


def stencil(extended, field, rate, wet):
    edge_sum = (
        extended[..., :-2, 1:-1]
        + extended[..., 2:, 1:-1]
        + extended[..., 1:-1, :-2]
        + extended[..., 1:-1, 2:]
    )
    diag_sum = (
        extended[..., :-2, :-2]
        + extended[..., :-2, 2:]
        + extended[..., 2:, :-2]
        + extended[..., 2:, 2:]
    )
    return wet * ((1.0 - 6.0 * rate) * field + rate * edge_sum + 0.5 * rate * diag_sum)


def horizontal(field, rate, wet, codes):
    count = lax.axis_size("tile")
    corner_set = jnp.stack(
        [field[..., 0, 0], field[..., 0, -1], field[..., -1, 0], field[..., -1, -1]], axis=-1
    )
    side = jnp.concatenate([field[..., :, 0], field[..., :, -1], corner_set], axis=-1)
    from_west = lax.ppermute(side, "tile", slot_pairs(count, 2))
    from_east = lax.ppermute(side, "tile", slot_pairs(count, 3))
    cols = field.shape[-1]
    rows = field.shape[-2]
    span = 2 * rows
    upright = jnp.concatenate(
        [field[..., 0, :], field[..., -1, :], from_west[..., span:], from_east[..., span:]], axis=-1
    )
    from_south = lax.ppermute(upright, "tile", slot_pairs(count, 0))
    from_north = lax.ppermute(upright, "tile", slot_pairs(count, 1))

    def strips(got, length):
        return jnp.stack([got[..., :length], got[..., length : 2 * length]], axis=-2)

    south = pick(strips(from_south, cols), codes[0])
    north = pick(strips(from_north, cols), codes[1])
    west = pick(strips(from_west, rows), codes[2])
    east = pick(strips(from_east, rows), codes[3])
    base = 2 * cols
    sources = [
        (from_south, base),
        (from_south, base + 4),
        (from_north, base),
        (from_north, base + 4),
    ]
    corners = []
    for slot, (got, first) in zip(range(4, 8), sources):
        code = codes[slot]
        cell = got[..., first : first + 4]
        value = jnp.where(
            code == 0,
            cell[..., 0],
            jnp.where(code == 1, cell[..., 1], jnp.where(code == 2, cell[..., 2], cell[..., 3])),
        )
        corners.append(value)
    middle = jnp.concatenate([west[..., None], field, east[..., None]], axis=-1)
    top_row = jnp.concatenate([corners[0][..., None], south, corners[1][..., None]], axis=-1)
    bottom_row = jnp.concatenate([corners[2][..., None], north, corners[3][..., None]], axis=-1)
    extended = jnp.concatenate([top_row[..., None, :], middle, bottom_row[..., None, :]], axis=-2)
    return stencil(extended, field, rate, wet)


def lev_exchange(outgoing):
    parts = outgoing.shape[0]
    here = lax.axis_index("lev")
    by_shift = [lax.dynamic_index_in_dim(outgoing, here, axis=0, keepdims=False)]
    for shift in range(1, parts):
        sent = lax.dynamic_index_in_dim(outgoing, (here + shift) % parts, axis=0, keepdims=False)
        pairs = [(source, (source + shift) % parts) for source in range(parts)]
        by_shift.append(lax.ppermute(sent, "lev", pairs))
    order = (here - jnp.arange(parts)) % parts
    return jnp.take(jnp.stack(by_shift), order, axis=0)


def column_mix(lateral, stacked_inverse, convective_rows):
    parts = lax.axis_size("lev")
    tracers, depth, rows, cols = lateral.shape
    part_rows = rows // parts
    outgoing = jnp.transpose(
        lateral.reshape(tracers, depth, parts, part_rows, cols), (2, 0, 1, 3, 4)
    )
    columns = lev_exchange(outgoing)
    mixed = []
    for tracer in range(tracers):
        flat = columns[:, tracer].reshape(parts * depth, part_rows * cols)
        both_states = jnp.dot(
            stacked_inverse[tracer], flat, precision=lax.Precision.HIGHEST
        ).reshape(2, parts, depth, part_rows, cols)
        mixed.append(jnp.where(convective_rows[None, None], both_states[1], both_states[0]))
    returning = lev_exchange(jnp.stack(mixed, axis=1))
    return jnp.transpose(returning, (1, 2, 0, 3, 4)).reshape(tracers, depth, rows, cols)


def local(forcing, lateral_mix, sea_mask, convective, mixing_inverse, seam_links):
    wet = sea_mask.astype(jnp.float32)[None]
    plane_rate = jnp.tile(lateral_mix, forcing.shape[0])[:, None, None]
    codes = seam_links[0] % 4
    parts = lax.axis_size("lev")
    rows = forcing.shape[2] // parts
    lev_here = lax.axis_index("lev")
    convective_rows = lax.dynamic_slice_in_dim(convective, lev_here * rows, rows, axis=0) == 1
    stacked_inverse = jnp.swapaxes(mixing_inverse, 2, 3).reshape(
        mixing_inverse.shape[0], -1, mixing_inverse.shape[2]
    )
    tracers, depth, rows, cols = forcing.shape
    adjoint = forcing
    for step in range(STEPS):
        planes = adjoint.reshape(tracers * depth, rows, cols)
        lateral = horizontal(planes, plane_rate, wet, codes)
        adjoint = column_mix(lateral.reshape(tracers, depth, rows, cols), stacked_inverse, convective_rows)
    return adjoint


def solution(mesh):
    return jax.shard_map(
        local,
        mesh=mesh,
        in_specs=(
            P(None, "lev", "tile", None),
            P("lev"),
            P("tile", None),
            P("tile", None),
            P(),
            P("tile", None),
        ),
        out_specs=P(None, "lev", "tile", None),
        check_vma=False,
    )
```

```python
import jax
import jax.numpy as jnp
from jax import lax
from jax.sharding import PartitionSpec as P

STEPS = 2
GRID_ROWS = 8

SLOT_STEPS = ((-1, 0), (1, 0), (0, -1), (0, 1), (-1, -1), (-1, 1), (1, -1), (1, 1))


def slot_pairs(count, slot):
    width = count // GRID_ROWS
    row_move, col_move = SLOT_STEPS[slot]
    pairs = []
    for target in range(count):
        row, col = divmod(target, width)
        source = ((row + row_move) % GRID_ROWS) * width + (col + col_move) % width
        pairs.append((source, target))
    return pairs


def pick(pair, code):
    strip = jnp.where(code % 2 == 0, pair[..., 0, :], pair[..., 1, :])
    return jnp.where(code // 2 == 1, strip[..., ::-1], strip)


def stencil(extended, field, rate, wet):
    edge_sum = (
        extended[..., :-2, 1:-1]
        + extended[..., 2:, 1:-1]
        + extended[..., 1:-1, :-2]
        + extended[..., 1:-1, 2:]
    )
    diag_sum = (
        extended[..., :-2, :-2]
        + extended[..., :-2, 2:]
        + extended[..., 2:, :-2]
        + extended[..., 2:, 2:]
    )
    return wet * ((1.0 - 6.0 * rate) * field + rate * edge_sum + 0.5 * rate * diag_sum)


def horizontal(field, rate, wet, codes):
    count = lax.axis_size("tile")
    corner_set = jnp.stack(
        [field[..., 0, 0], field[..., 0, -1], field[..., -1, 0], field[..., -1, -1]], axis=-1
    )
    side = jnp.concatenate([field[..., :, 0], field[..., :, -1], corner_set], axis=-1)
    from_west = lax.ppermute(side, "tile", slot_pairs(count, 2))
    from_east = lax.ppermute(side, "tile", slot_pairs(count, 3))
    cols = field.shape[-1]
    rows = field.shape[-2]
    span = 2 * rows
    upright = jnp.concatenate(
        [field[..., 0, :], field[..., -1, :], from_west[..., span:], from_east[..., span:]], axis=-1
    )
    from_south = lax.ppermute(upright, "tile", slot_pairs(count, 0))
    from_north = lax.ppermute(upright, "tile", slot_pairs(count, 1))

    def strips(got, length):
        return jnp.stack([got[..., :length], got[..., length : 2 * length]], axis=-2)

    south = pick(strips(from_south, cols), codes[0])
    north = pick(strips(from_north, cols), codes[1])
    west = pick(strips(from_west, rows), codes[2])
    east = pick(strips(from_east, rows), codes[3])
    base = 2 * cols
    sources = [
        (from_south, base),
        (from_south, base + 4),
        (from_north, base),
        (from_north, base + 4),
    ]
    corners = []
    for slot, (got, first) in zip(range(4, 8), sources):
        code = codes[slot]
        cell = got[..., first : first + 4]
        value = jnp.where(
            code == 0,
            cell[..., 0],
            jnp.where(code == 1, cell[..., 1], jnp.where(code == 2, cell[..., 2], cell[..., 3])),
        )
        corners.append(value)
    middle = jnp.concatenate([west[..., None], field, east[..., None]], axis=-1)
    top_row = jnp.concatenate([corners[0][..., None], south, corners[1][..., None]], axis=-1)
    bottom_row = jnp.concatenate([corners[2][..., None], north, corners[3][..., None]], axis=-1)
    extended = jnp.concatenate([top_row[..., None, :], middle, bottom_row[..., None, :]], axis=-2)
    return stencil(extended, field, rate, wet)


def to_rows(lateral):
    parts = lax.axis_size("lev")
    tracers, depth, rows, cols = lateral.shape
    part_rows = rows // parts
    outgoing = jnp.transpose(
        lateral.reshape(tracers, depth, parts, part_rows, cols), (2, 0, 1, 3, 4)
    )
    columns = lax.all_to_all(outgoing, "lev", 0, 0, tiled=True)
    return jnp.transpose(columns, (1, 0, 2, 3, 4)).reshape(tracers, parts * depth, part_rows, cols)


def to_levels(block):
    parts = lax.axis_size("lev")
    tracers, levels, part_rows, cols = block.shape
    depth = levels // parts
    outgoing = jnp.transpose(block.reshape(tracers, parts, depth, part_rows, cols), (1, 0, 2, 3, 4))
    returning = lax.all_to_all(outgoing, "lev", 0, 0, tiled=True)
    return jnp.transpose(returning, (1, 2, 0, 3, 4)).reshape(tracers, depth, parts * part_rows, cols)


def column_mix(block, stacked_inverse, convective_rows):
    tracers, levels, part_rows, cols = block.shape
    mixed = []
    for tracer in range(tracers):
        flat = block[tracer].reshape(levels, part_rows * cols)
        both_states = jnp.dot(
            stacked_inverse[tracer], flat, precision=lax.Precision.HIGHEST
        ).reshape(2, levels, part_rows, cols)
        mixed.append(jnp.where(convective_rows[None], both_states[1], both_states[0]))
    return jnp.stack(mixed)


def horizontal_rows(block, rate, wet, codes):
    count = lax.axis_size("tile")
    parts = lax.axis_size("lev")
    part = lax.axis_index("lev")
    planes, part_rows, cols = block.shape
    rows = parts * part_rows
    own = jnp.concatenate(
        [block[:, 0, :], block[:, -1, :], block[:, :, 0], block[:, :, -1]], axis=-1
    )
    gathered = lax.all_gather(own, "lev")
    first_row = gathered[0, :, :cols]
    last_row = gathered[parts - 1, :, cols : 2 * cols]

    def column(offset):
        pieces = gathered[:, :, 2 * cols + offset : 2 * cols + offset + part_rows]
        return jnp.transpose(pieces, (1, 0, 2)).reshape(planes, rows)

    first_col = column(0)
    last_col = column(part_rows)
    corner_set = jnp.stack(
        [first_row[:, 0], first_row[:, -1], last_row[:, 0], last_row[:, -1]], axis=-1
    )
    side = jnp.concatenate([first_col, last_col, corner_set], axis=-1)
    from_west = lax.ppermute(side, "tile", slot_pairs(count, 2))
    from_east = lax.ppermute(side, "tile", slot_pairs(count, 3))
    span = 2 * rows
    upright = jnp.concatenate(
        [first_row, last_row, from_west[..., span:], from_east[..., span:]], axis=-1
    )
    from_south = lax.ppermute(upright, "tile", slot_pairs(count, 0))
    from_north = lax.ppermute(upright, "tile", slot_pairs(count, 1))

    def strips(got, length):
        return jnp.stack([got[..., :length], got[..., length : 2 * length]], axis=-2)

    def corner(got, first, code):
        cell = got[..., first : first + 4]
        return jnp.where(
            code == 0,
            cell[..., 0],
            jnp.where(code == 1, cell[..., 1], jnp.where(code == 2, cell[..., 2], cell[..., 3])),
        )

    south = pick(strips(from_south, cols), codes[0])
    north = pick(strips(from_north, cols), codes[1])
    west = pick(strips(from_west, rows), codes[2])
    east = pick(strips(from_east, rows), codes[3])
    base = 2 * cols
    west_full = jnp.concatenate(
        [corner(from_south, base, codes[4])[:, None], west, corner(from_north, base, codes[6])[:, None]],
        axis=-1,
    )
    east_full = jnp.concatenate(
        [corner(from_south, base + 4, codes[5])[:, None], east, corner(from_north, base + 4, codes[7])[:, None]],
        axis=-1,
    )
    west_part = lax.dynamic_slice_in_dim(west_full, part * part_rows, part_rows + 2, axis=1)
    east_part = lax.dynamic_slice_in_dim(east_full, part * part_rows, part_rows + 2, axis=1)
    before = lax.dynamic_index_in_dim(gathered, (part + parts - 1) % parts, axis=0, keepdims=False)
    after = lax.dynamic_index_in_dim(gathered, (part + 1) % parts, axis=0, keepdims=False)
    above = jnp.where(part == 0, south, before[:, cols : 2 * cols])
    below = jnp.where(part == parts - 1, north, after[:, :cols])
    middle = jnp.concatenate([above[:, None, :], block, below[:, None, :]], axis=1)
    extended = jnp.concatenate([west_part[:, :, None], middle, east_part[:, :, None]], axis=2)
    return stencil(extended, block, rate, wet)


def local(forcing, lateral_mix, sea_mask, convective, mixing_inverse, seam_links):
    tracers, depth, rows, cols = forcing.shape
    parts = lax.axis_size("lev")
    part_rows = rows // parts
    part = lax.axis_index("lev")
    codes = seam_links[0] % 4
    wet = sea_mask.astype(jnp.float32)[None]
    plane_rate = jnp.tile(lateral_mix, tracers)[:, None, None]
    all_rates = lax.all_gather(lateral_mix, "lev", tiled=True)
    block_rate = jnp.tile(all_rates, tracers)[:, None, None]
    wet_rows = lax.dynamic_slice_in_dim(wet, part * part_rows, part_rows, axis=1)
    convective_rows = lax.dynamic_slice_in_dim(convective, part * part_rows, part_rows, axis=0) == 1
    stacked_inverse = jnp.swapaxes(mixing_inverse, 2, 3).reshape(
        mixing_inverse.shape[0], -1, mixing_inverse.shape[2]
    )
    lateral = horizontal(forcing.reshape(tracers * depth, rows, cols), plane_rate, wet, codes)
    block = column_mix(to_rows(lateral.reshape(tracers, depth, rows, cols)), stacked_inverse, convective_rows)
    levels = block.shape[1]
    for step in range(1, STEPS):
        lateral = horizontal_rows(block.reshape(tracers * levels, part_rows, cols), block_rate, wet_rows, codes)
        block = column_mix(lateral.reshape(tracers, levels, part_rows, cols), stacked_inverse, convective_rows)
    return to_levels(block)


def solution(mesh):
    return jax.shard_map(
        local,
        mesh=mesh,
        in_specs=(
            P(None, "lev", "tile", None),
            P("lev"),
            P("tile", None),
            P("tile", None),
            P(),
            P("tile", None),
        ),
        out_specs=P(None, "lev", "tile", None),
        check_vma=False,
    )
```

```python
import jax
import jax.numpy as jnp
from jax import lax
from jax.sharding import PartitionSpec as P

STEPS = 2
GRID_ROWS = 8

SLOT_STEPS = ((-1, 0), (1, 0), (0, -1), (0, 1), (-1, -1), (-1, 1), (1, -1), (1, 1))


def slot_pairs(count, slot):
    width = count // GRID_ROWS
    row_move, col_move = SLOT_STEPS[slot]
    pairs = []
    for target in range(count):
        row, col = divmod(target, width)
        source = ((row + row_move) % GRID_ROWS) * width + (col + col_move) % width
        pairs.append((source, target))
    return pairs


def pick(pair, code):
    strip = jnp.where(code % 2 == 0, pair[..., 0, :], pair[..., 1, :])
    return jnp.where(code // 2 == 1, strip[..., ::-1], strip)


def stencil(extended, field, rate, wet):
    edge_sum = (
        extended[..., :-2, 1:-1]
        + extended[..., 2:, 1:-1]
        + extended[..., 1:-1, :-2]
        + extended[..., 1:-1, 2:]
    )
    diag_sum = (
        extended[..., :-2, :-2]
        + extended[..., :-2, 2:]
        + extended[..., 2:, :-2]
        + extended[..., 2:, 2:]
    )
    return wet * ((1.0 - 6.0 * rate) * field + rate * edge_sum + 0.5 * rate * diag_sum)


def horizontal(field, rate, wet, codes):
    count = lax.axis_size("tile")
    corner_set = jnp.stack(
        [field[..., 0, 0], field[..., 0, -1], field[..., -1, 0], field[..., -1, -1]], axis=-1
    )
    side = jnp.concatenate([field[..., :, 0], field[..., :, -1], corner_set], axis=-1)
    from_west = lax.ppermute(side, "tile", slot_pairs(count, 2))
    from_east = lax.ppermute(side, "tile", slot_pairs(count, 3))
    cols = field.shape[-1]
    rows = field.shape[-2]
    span = 2 * rows
    upright = jnp.concatenate(
        [field[..., 0, :], field[..., -1, :], from_west[..., span:], from_east[..., span:]], axis=-1
    )
    from_south = lax.ppermute(upright, "tile", slot_pairs(count, 0))
    from_north = lax.ppermute(upright, "tile", slot_pairs(count, 1))

    def strips(got, length):
        return jnp.stack([got[..., :length], got[..., length : 2 * length]], axis=-2)

    south = pick(strips(from_south, cols), codes[0])
    north = pick(strips(from_north, cols), codes[1])
    west = pick(strips(from_west, rows), codes[2])
    east = pick(strips(from_east, rows), codes[3])
    base = 2 * cols
    sources = [
        (from_south, base),
        (from_south, base + 4),
        (from_north, base),
        (from_north, base + 4),
    ]
    corners = []
    for slot, (got, first) in zip(range(4, 8), sources):
        code = codes[slot]
        cell = got[..., first : first + 4]
        value = jnp.where(
            code == 0,
            cell[..., 0],
            jnp.where(code == 1, cell[..., 1], jnp.where(code == 2, cell[..., 2], cell[..., 3])),
        )
        corners.append(value)
    middle = jnp.concatenate([west[..., None], field, east[..., None]], axis=-1)
    top_row = jnp.concatenate([corners[0][..., None], south, corners[1][..., None]], axis=-1)
    bottom_row = jnp.concatenate([corners[2][..., None], north, corners[3][..., None]], axis=-1)
    extended = jnp.concatenate([top_row[..., None, :], middle, bottom_row[..., None, :]], axis=-2)
    return stencil(extended, field, rate, wet)


def to_rows(lateral):
    parts = lax.axis_size("lev")
    tracers, depth, rows, cols = lateral.shape
    part_rows = rows // parts
    padded = jnp.pad(lateral, ((0, 0), (0, 0), (1, 1), (0, 0)))
    edges = jnp.concatenate(
        [lateral[..., :, 0], lateral[..., :, -1], lateral[..., 0, :], lateral[..., -1, :]], axis=-1
    )
    outgoing = []
    for dest in range(parts):
        window = padded[:, :, dest * part_rows : dest * part_rows + part_rows + 2, :]
        outgoing.append(
            jnp.concatenate([window.reshape(tracers, depth, (part_rows + 2) * cols), edges], axis=-1)
        )
    columns = lax.all_to_all(jnp.stack(outgoing), "lev", 0, 0, tiled=True)
    return jnp.transpose(columns, (1, 0, 2, 3)).reshape(tracers, parts * depth, -1)


def to_levels(block):
    parts = lax.axis_size("lev")
    tracers, levels, part_rows, cols = block.shape
    depth = levels // parts
    outgoing = jnp.transpose(block.reshape(tracers, parts, depth, part_rows, cols), (1, 0, 2, 3, 4))
    returning = lax.all_to_all(outgoing, "lev", 0, 0, tiled=True)
    return jnp.transpose(returning, (1, 2, 0, 3, 4)).reshape(tracers, depth, parts * part_rows, cols)


def column_mix(block, stacked_inverse, convective_map):
    tracers, levels, width = block.shape
    mixed = []
    for tracer in range(tracers):
        both_states = jnp.dot(
            stacked_inverse[tracer], block[tracer], precision=lax.Precision.HIGHEST
        ).reshape(2, levels, width)
        mixed.append(jnp.where(convective_map[None], both_states[1], both_states[0]))
    return jnp.stack(mixed)


def horizontal_rows(halo_block, edges, rate, wet, codes):
    count = lax.axis_size("tile")
    parts = lax.axis_size("lev")
    part = lax.axis_index("lev")
    planes, halo_rows, cols = halo_block.shape
    part_rows = halo_rows - 2
    rows = parts * part_rows
    block = halo_block[:, 1:-1, :]
    first_col = edges[:, :rows]
    last_col = edges[:, rows : 2 * rows]
    first_row = edges[:, 2 * rows : 2 * rows + cols]
    last_row = edges[:, 2 * rows + cols :]
    corner_set = jnp.stack(
        [first_row[:, 0], first_row[:, -1], last_row[:, 0], last_row[:, -1]], axis=-1
    )
    side = jnp.concatenate([first_col, last_col, corner_set], axis=-1)
    from_west = lax.ppermute(side, "tile", slot_pairs(count, 2))
    from_east = lax.ppermute(side, "tile", slot_pairs(count, 3))
    span = 2 * rows
    upright = jnp.concatenate(
        [first_row, last_row, from_west[..., span:], from_east[..., span:]], axis=-1
    )
    from_south = lax.ppermute(upright, "tile", slot_pairs(count, 0))
    from_north = lax.ppermute(upright, "tile", slot_pairs(count, 1))

    def strips(got, length):
        return jnp.stack([got[..., :length], got[..., length : 2 * length]], axis=-2)

    def corner(got, first, code):
        cell = got[..., first : first + 4]
        return jnp.where(
            code == 0,
            cell[..., 0],
            jnp.where(code == 1, cell[..., 1], jnp.where(code == 2, cell[..., 2], cell[..., 3])),
        )

    south = pick(strips(from_south, cols), codes[0])
    north = pick(strips(from_north, cols), codes[1])
    west = pick(strips(from_west, rows), codes[2])
    east = pick(strips(from_east, rows), codes[3])
    base = 2 * cols
    west_full = jnp.concatenate(
        [corner(from_south, base, codes[4])[:, None], west, corner(from_north, base, codes[6])[:, None]],
        axis=-1,
    )
    east_full = jnp.concatenate(
        [corner(from_south, base + 4, codes[5])[:, None], east, corner(from_north, base + 4, codes[7])[:, None]],
        axis=-1,
    )
    west_part = lax.dynamic_slice_in_dim(west_full, part * part_rows, part_rows + 2, axis=1)
    east_part = lax.dynamic_slice_in_dim(east_full, part * part_rows, part_rows + 2, axis=1)
    above = jnp.where(part == 0, south, halo_block[:, 0, :])
    below = jnp.where(part == parts - 1, north, halo_block[:, -1, :])
    middle = jnp.concatenate([above[:, None, :], block, below[:, None, :]], axis=1)
    extended = jnp.concatenate([west_part[:, :, None], middle, east_part[:, :, None]], axis=2)
    return stencil(extended, block, rate, wet)


def local(forcing, lateral_mix, sea_mask, convective, mixing_inverse, seam_links):
    tracers, depth, rows, cols = forcing.shape
    parts = lax.axis_size("lev")
    part_rows = rows // parts
    part = lax.axis_index("lev")
    codes = seam_links[0] % 4
    wet = sea_mask.astype(jnp.float32)[None]
    plane_rate = jnp.tile(lateral_mix, tracers)[:, None, None]
    all_rates = lax.all_gather(lateral_mix, "lev", tiled=True)
    block_rate = jnp.tile(all_rates, tracers)[:, None, None]
    wet_rows = lax.dynamic_slice_in_dim(wet, part * part_rows, part_rows, axis=1)
    is_convective = convective == 1
    halo_convective = lax.dynamic_slice_in_dim(
        jnp.pad(is_convective, ((1, 1), (0, 0))), part * part_rows, part_rows + 2, axis=0
    )
    first_map = jnp.concatenate(
        [
            halo_convective.reshape(-1),
            is_convective[:, 0],
            is_convective[:, -1],
            is_convective[0, :],
            is_convective[-1, :],
        ]
    )
    convective_rows = lax.dynamic_slice_in_dim(
        is_convective, part * part_rows, part_rows, axis=0
    ).reshape(-1)
    stacked_inverse = jnp.swapaxes(mixing_inverse, 2, 3).reshape(
        mixing_inverse.shape[0], -1, mixing_inverse.shape[2]
    )
    lateral = horizontal(forcing.reshape(tracers * depth, rows, cols), plane_rate, wet, codes)
    mixed = column_mix(to_rows(lateral.reshape(tracers, depth, rows, cols)), stacked_inverse, first_map)
    levels = mixed.shape[1]
    halo_width = (part_rows + 2) * cols
    halo_block = mixed[:, :, :halo_width].reshape(tracers * levels, part_rows + 2, cols)
    edges = mixed[:, :, halo_width:].reshape(tracers * levels, -1)
    lateral = horizontal_rows(halo_block, edges, block_rate, wet_rows, codes)
    block = column_mix(
        lateral.reshape(tracers, levels, part_rows * cols), stacked_inverse, convective_rows
    )
    return to_levels(block.reshape(tracers, levels, part_rows, cols))


def solution(mesh):
    return jax.shard_map(
        local,
        mesh=mesh,
        in_specs=(
            P(None, "lev", "tile", None),
            P("lev"),
            P("tile", None),
            P("tile", None),
            P(),
            P("tile", None),
        ),
        out_specs=P(None, "lev", "tile", None),
        check_vma=False,
    )
```

```python
import jax
import jax.numpy as jnp
from jax import lax
from jax.sharding import PartitionSpec as P

STEPS = 2
GRID_ROWS = 8

SLOT_STEPS = ((-1, 0), (1, 0), (0, -1), (0, 1), (-1, -1), (-1, 1), (1, -1), (1, 1))


def slot_pairs(count, slot):
    width = count // GRID_ROWS
    row_move, col_move = SLOT_STEPS[slot]
    pairs = []
    for target in range(count):
        row, col = divmod(target, width)
        source = ((row + row_move) % GRID_ROWS) * width + (col + col_move) % width
        pairs.append((source, target))
    return pairs


def pick(pair, code):
    strip = jnp.where(code % 2 == 0, pair[..., 0, :], pair[..., 1, :])
    return jnp.where(code // 2 == 1, strip[..., ::-1], strip)


def stencil(extended, field, rate, wet):
    edge_sum = (
        extended[..., :-2, 1:-1]
        + extended[..., 2:, 1:-1]
        + extended[..., 1:-1, :-2]
        + extended[..., 1:-1, 2:]
    )
    diag_sum = (
        extended[..., :-2, :-2]
        + extended[..., :-2, 2:]
        + extended[..., 2:, :-2]
        + extended[..., 2:, 2:]
    )
    return wet * ((1.0 - 6.0 * rate) * field + rate * edge_sum + 0.5 * rate * diag_sum)


def horizontal(field, rate, wet, codes):
    count = lax.axis_size("tile")
    corner_set = jnp.stack(
        [field[..., 0, 0], field[..., 0, -1], field[..., -1, 0], field[..., -1, -1]], axis=-1
    )
    side = jnp.concatenate([field[..., :, 0], field[..., :, -1], corner_set], axis=-1)
    from_west = lax.ppermute(side, "tile", slot_pairs(count, 2))
    from_east = lax.ppermute(side, "tile", slot_pairs(count, 3))
    cols = field.shape[-1]
    rows = field.shape[-2]
    span = 2 * rows
    upright = jnp.concatenate(
        [field[..., 0, :], field[..., -1, :], from_west[..., span:], from_east[..., span:]], axis=-1
    )
    from_south = lax.ppermute(upright, "tile", slot_pairs(count, 0))
    from_north = lax.ppermute(upright, "tile", slot_pairs(count, 1))

    def strips(got, length):
        return jnp.stack([got[..., :length], got[..., length : 2 * length]], axis=-2)

    south = pick(strips(from_south, cols), codes[0])
    north = pick(strips(from_north, cols), codes[1])
    west = pick(strips(from_west, rows), codes[2])
    east = pick(strips(from_east, rows), codes[3])
    base = 2 * cols
    sources = [
        (from_south, base),
        (from_south, base + 4),
        (from_north, base),
        (from_north, base + 4),
    ]
    corners = []
    for slot, (got, first) in zip(range(4, 8), sources):
        code = codes[slot]
        cell = got[..., first : first + 4]
        value = jnp.where(
            code == 0,
            cell[..., 0],
            jnp.where(code == 1, cell[..., 1], jnp.where(code == 2, cell[..., 2], cell[..., 3])),
        )
        corners.append(value)
    middle = jnp.concatenate([west[..., None], field, east[..., None]], axis=-1)
    top_row = jnp.concatenate([corners[0][..., None], south, corners[1][..., None]], axis=-1)
    bottom_row = jnp.concatenate([corners[2][..., None], north, corners[3][..., None]], axis=-1)
    extended = jnp.concatenate([top_row[..., None, :], middle, bottom_row[..., None, :]], axis=-2)
    return stencil(extended, field, rate, wet)


def to_rows(lateral, rate):
    parts = lax.axis_size("lev")
    tracers, depth, rows, cols = lateral.shape
    part_rows = rows // parts
    padded = jnp.pad(lateral, ((0, 0), (0, 0), (1, 1), (0, 0)))
    rate_column = jnp.broadcast_to(rate[None, :, None], (tracers, depth, 1))
    edges = jnp.concatenate(
        [lateral[..., :, 0], lateral[..., :, -1], lateral[..., 0, :], lateral[..., -1, :], rate_column],
        axis=-1,
    )
    outgoing = []
    for dest in range(parts):
        window = padded[:, :, dest * part_rows : dest * part_rows + part_rows + 2, :]
        outgoing.append(
            jnp.concatenate([window.reshape(tracers, depth, (part_rows + 2) * cols), edges], axis=-1)
        )
    columns = lax.all_to_all(jnp.stack(outgoing), "lev", 0, 0, tiled=True)
    gathered = jnp.transpose(columns, (1, 0, 2, 3)).reshape(tracers, parts * depth, -1)
    return gathered[..., :-1], gathered[0, :, -1]


def to_levels(block):
    parts = lax.axis_size("lev")
    tracers, levels, part_rows, cols = block.shape
    depth = levels // parts
    outgoing = jnp.transpose(block.reshape(tracers, parts, depth, part_rows, cols), (1, 0, 2, 3, 4))
    returning = lax.all_to_all(outgoing, "lev", 0, 0, tiled=True)
    return jnp.transpose(returning, (1, 2, 0, 3, 4)).reshape(tracers, depth, parts * part_rows, cols)


def column_mix(block, stacked_inverse, convective_map):
    tracers, levels, width = block.shape
    mixed = []
    for tracer in range(tracers):
        both_states = jnp.dot(
            stacked_inverse[tracer], block[tracer], precision=lax.Precision.HIGHEST
        ).reshape(2, levels, width)
        mixed.append(jnp.where(convective_map[None], both_states[1], both_states[0]))
    return jnp.stack(mixed)


def horizontal_rows(halo_block, edges, rate, wet, codes):
    count = lax.axis_size("tile")
    parts = lax.axis_size("lev")
    part = lax.axis_index("lev")
    planes, halo_rows, cols = halo_block.shape
    part_rows = halo_rows - 2
    rows = parts * part_rows
    block = halo_block[:, 1:-1, :]
    first_col = edges[:, :rows]
    last_col = edges[:, rows : 2 * rows]
    first_row = edges[:, 2 * rows : 2 * rows + cols]
    last_row = edges[:, 2 * rows + cols :]
    corner_set = jnp.stack(
        [first_row[:, 0], first_row[:, -1], last_row[:, 0], last_row[:, -1]], axis=-1
    )
    side = jnp.concatenate([first_col, last_col, corner_set], axis=-1)
    from_west = lax.ppermute(side, "tile", slot_pairs(count, 2))
    from_east = lax.ppermute(side, "tile", slot_pairs(count, 3))
    span = 2 * rows
    upright = jnp.concatenate(
        [first_row, last_row, from_west[..., span:], from_east[..., span:]], axis=-1
    )
    from_south = lax.ppermute(upright, "tile", slot_pairs(count, 0))
    from_north = lax.ppermute(upright, "tile", slot_pairs(count, 1))

    def strips(got, length):
        return jnp.stack([got[..., :length], got[..., length : 2 * length]], axis=-2)

    def corner(got, first, code):
        cell = got[..., first : first + 4]
        return jnp.where(
            code == 0,
            cell[..., 0],
            jnp.where(code == 1, cell[..., 1], jnp.where(code == 2, cell[..., 2], cell[..., 3])),
        )

    south = pick(strips(from_south, cols), codes[0])
    north = pick(strips(from_north, cols), codes[1])
    west = pick(strips(from_west, rows), codes[2])
    east = pick(strips(from_east, rows), codes[3])
    base = 2 * cols
    west_full = jnp.concatenate(
        [corner(from_south, base, codes[4])[:, None], west, corner(from_north, base, codes[6])[:, None]],
        axis=-1,
    )
    east_full = jnp.concatenate(
        [corner(from_south, base + 4, codes[5])[:, None], east, corner(from_north, base + 4, codes[7])[:, None]],
        axis=-1,
    )
    west_part = lax.dynamic_slice_in_dim(west_full, part * part_rows, part_rows + 2, axis=1)
    east_part = lax.dynamic_slice_in_dim(east_full, part * part_rows, part_rows + 2, axis=1)
    above = jnp.where(part == 0, south, halo_block[:, 0, :])
    below = jnp.where(part == parts - 1, north, halo_block[:, -1, :])
    middle = jnp.concatenate([above[:, None, :], block, below[:, None, :]], axis=1)
    extended = jnp.concatenate([west_part[:, :, None], middle, east_part[:, :, None]], axis=2)
    return stencil(extended, block, rate, wet)


def local(forcing, lateral_mix, sea_mask, convective, mixing_inverse, seam_links):
    tracers, depth, rows, cols = forcing.shape
    parts = lax.axis_size("lev")
    part_rows = rows // parts
    part = lax.axis_index("lev")
    codes = seam_links[0] % 4
    wet = sea_mask.astype(jnp.float32)[None]
    plane_rate = jnp.tile(lateral_mix, tracers)[:, None, None]
    wet_rows = lax.dynamic_slice_in_dim(wet, part * part_rows, part_rows, axis=1)
    is_convective = convective == 1
    halo_convective = lax.dynamic_slice_in_dim(
        jnp.pad(is_convective, ((1, 1), (0, 0))), part * part_rows, part_rows + 2, axis=0
    )
    first_map = jnp.concatenate(
        [
            halo_convective.reshape(-1),
            is_convective[:, 0],
            is_convective[:, -1],
            is_convective[0, :],
            is_convective[-1, :],
        ]
    )
    convective_rows = lax.dynamic_slice_in_dim(
        is_convective, part * part_rows, part_rows, axis=0
    ).reshape(-1)
    stacked_inverse = jnp.swapaxes(mixing_inverse, 2, 3).reshape(
        mixing_inverse.shape[0], -1, mixing_inverse.shape[2]
    )
    lateral = horizontal(forcing.reshape(tracers * depth, rows, cols), plane_rate, wet, codes)
    gathered, all_rates = to_rows(lateral.reshape(tracers, depth, rows, cols), lateral_mix)
    block_rate = jnp.tile(all_rates, tracers)[:, None, None]
    mixed = column_mix(gathered, stacked_inverse, first_map)
    levels = mixed.shape[1]
    halo_width = (part_rows + 2) * cols
    halo_block = mixed[:, :, :halo_width].reshape(tracers * levels, part_rows + 2, cols)
    edges = mixed[:, :, halo_width:].reshape(tracers * levels, -1)
    lateral = horizontal_rows(halo_block, edges, block_rate, wet_rows, codes)
    block = column_mix(
        lateral.reshape(tracers, levels, part_rows * cols), stacked_inverse, convective_rows
    )
    return to_levels(block.reshape(tracers, levels, part_rows, cols))


def solution(mesh):
    return jax.shard_map(
        local,
        mesh=mesh,
        in_specs=(
            P(None, "lev", "tile", None),
            P("lev"),
            P("tile", None),
            P("tile", None),
            P(),
            P("tile", None),
        ),
        out_specs=P(None, "lev", "tile", None),
        check_vma=False,
    )
```

```python
import jax
import jax.numpy as jnp
from jax import lax
from jax.sharding import PartitionSpec as P

STEPS = 2
GRID_ROWS = 8

SLOT_STEPS = ((-1, 0), (1, 0), (0, -1), (0, 1), (-1, -1), (-1, 1), (1, -1), (1, 1))


def slot_pairs(count, slot):
    width = count // GRID_ROWS
    row_move, col_move = SLOT_STEPS[slot]
    pairs = []
    for target in range(count):
        row, col = divmod(target, width)
        source = ((row + row_move) % GRID_ROWS) * width + (col + col_move) % width
        pairs.append((source, target))
    return pairs


def pick(pair, code):
    strip = jnp.where(code % 2 == 0, pair[..., 0, :], pair[..., 1, :])
    return jnp.where(code // 2 == 1, strip[..., ::-1], strip)


def stencil(extended, field, rate, wet):
    edge_sum = (
        extended[..., :-2, 1:-1]
        + extended[..., 2:, 1:-1]
        + extended[..., 1:-1, :-2]
        + extended[..., 1:-1, 2:]
    )
    diag_sum = (
        extended[..., :-2, :-2]
        + extended[..., :-2, 2:]
        + extended[..., 2:, :-2]
        + extended[..., 2:, 2:]
    )
    return wet * ((1.0 - 6.0 * rate) * field + rate * edge_sum + 0.5 * rate * diag_sum)


def horizontal(field, rate, wet, codes):
    count = lax.axis_size("tile")
    corner_set = jnp.stack(
        [field[..., 0, 0], field[..., 0, -1], field[..., -1, 0], field[..., -1, -1]], axis=-1
    )
    side = jnp.concatenate([field[..., :, 0], field[..., :, -1], corner_set], axis=-1)
    from_west = lax.ppermute(side, "tile", slot_pairs(count, 2))
    from_east = lax.ppermute(side, "tile", slot_pairs(count, 3))
    cols = field.shape[-1]
    rows = field.shape[-2]
    span = 2 * rows
    upright = jnp.concatenate(
        [field[..., 0, :], field[..., -1, :], from_west[..., span:], from_east[..., span:]], axis=-1
    )
    from_south = lax.ppermute(upright, "tile", slot_pairs(count, 0))
    from_north = lax.ppermute(upright, "tile", slot_pairs(count, 1))

    def strips(got, length):
        return jnp.stack([got[..., :length], got[..., length : 2 * length]], axis=-2)

    south = pick(strips(from_south, cols), codes[0])
    north = pick(strips(from_north, cols), codes[1])
    west = pick(strips(from_west, rows), codes[2])
    east = pick(strips(from_east, rows), codes[3])
    base = 2 * cols
    sources = [
        (from_south, base),
        (from_south, base + 4),
        (from_north, base),
        (from_north, base + 4),
    ]
    corners = []
    for slot, (got, first) in zip(range(4, 8), sources):
        code = codes[slot]
        cell = got[..., first : first + 4]
        value = jnp.where(
            code == 0,
            cell[..., 0],
            jnp.where(code == 1, cell[..., 1], jnp.where(code == 2, cell[..., 2], cell[..., 3])),
        )
        corners.append(value)
    middle = jnp.concatenate([west[..., None], field, east[..., None]], axis=-1)
    top_row = jnp.concatenate([corners[0][..., None], south, corners[1][..., None]], axis=-1)
    bottom_row = jnp.concatenate([corners[2][..., None], north, corners[3][..., None]], axis=-1)
    extended = jnp.concatenate([top_row[..., None, :], middle, bottom_row[..., None, :]], axis=-2)
    return stencil(extended, field, rate, wet)


def to_rows(lateral, rate):
    parts = lax.axis_size("lev")
    tracers, depth, rows, cols = lateral.shape
    part_rows = rows // parts
    padded = jnp.pad(lateral, ((0, 0), (0, 0), (1, 1), (0, 0)))
    rate_column = jnp.broadcast_to(rate[None, :, None], (tracers, depth, 1))
    edges = jnp.concatenate(
        [lateral[..., :, 0], lateral[..., :, -1], lateral[..., 0, :], lateral[..., -1, :], rate_column],
        axis=-1,
    )
    outgoing = []
    for dest in range(parts):
        window = padded[:, :, dest * part_rows : dest * part_rows + part_rows + 2, :]
        outgoing.append(
            jnp.concatenate([window.reshape(tracers, depth, (part_rows + 2) * cols), edges], axis=-1)
        )
    columns = lax.all_to_all(jnp.stack(outgoing), "lev", 0, 0, tiled=True)
    gathered = jnp.transpose(columns, (1, 0, 2, 3)).reshape(tracers, parts * depth, -1)
    return gathered[..., :-1], gathered[0, :, -1]


def to_levels(block):
    parts = lax.axis_size("lev")
    tracers, levels, part_rows, cols = block.shape
    depth = levels // parts
    outgoing = jnp.transpose(block.reshape(tracers, parts, depth, part_rows, cols), (1, 0, 2, 3, 4))
    returning = lax.all_to_all(outgoing, "lev", 0, 0, tiled=True)
    return jnp.transpose(returning, (1, 2, 0, 3, 4)).reshape(tracers, depth, parts * part_rows, cols)


def column_mix(block, stacked_inverse, convective_map):
    tracers, levels, width = block.shape
    mixed = []
    for tracer in range(tracers):
        both_states = jnp.dot(
            stacked_inverse[tracer], block[tracer], precision=lax.Precision.HIGHEST
        ).reshape(2, levels, width)
        mixed.append(jnp.where(convective_map[None], both_states[1], both_states[0]))
    return jnp.stack(mixed)


def horizontal_rows(halo_block, edges, rate, wet, codes):
    count = lax.axis_size("tile")
    parts = lax.axis_size("lev")
    part = lax.axis_index("lev")
    planes, halo_rows, cols = halo_block.shape
    part_rows = halo_rows - 2
    rows = parts * part_rows
    block = halo_block[:, 1:-1, :]
    first_col = edges[:, :rows]
    last_col = edges[:, rows : 2 * rows]
    first_row = edges[:, 2 * rows : 2 * rows + cols]
    last_row = edges[:, 2 * rows + cols :]
    corner_set = jnp.stack(
        [first_row[:, 0], first_row[:, -1], last_row[:, 0], last_row[:, -1]], axis=-1
    )
    row_pair = jnp.concatenate([first_row, last_row], axis=-1)
    col_pair = jnp.pad(jnp.concatenate([first_col, last_col], axis=-1), ((0, 0), (0, 2 * (cols - rows))))
    strip_pair = jnp.where(part < 2, row_pair, col_pair)
    both = ("tile", "lev")

    def lifted(slot_of_part):
        return [
            (source * parts + lev, target * parts + lev)
            for lev in range(parts)
            for source, target in slot_pairs(count, slot_of_part(lev))
        ]

    got_strips = lax.ppermute(strip_pair, both, lifted(lambda lev: lev))
    got_corners = lax.ppermute(corner_set, both, lifted(lambda lev: 4 + lev))
    shared = lax.all_gather(jnp.concatenate([got_strips, got_corners], axis=-1), "lev")

    def strips(got, length):
        return jnp.stack([got[..., :length], got[..., length : 2 * length]], axis=-2)

    def corner(slot):
        cell = shared[slot - 4, :, 2 * cols : 2 * cols + 4]
        code = codes[slot]
        return jnp.where(
            code == 0,
            cell[..., 0],
            jnp.where(code == 1, cell[..., 1], jnp.where(code == 2, cell[..., 2], cell[..., 3])),
        )

    south = pick(strips(shared[0], cols), codes[0])
    north = pick(strips(shared[1], cols), codes[1])
    west = pick(strips(shared[2], rows), codes[2])
    east = pick(strips(shared[3], rows), codes[3])
    west_full = jnp.concatenate([corner(4)[:, None], west, corner(6)[:, None]], axis=-1)
    east_full = jnp.concatenate([corner(5)[:, None], east, corner(7)[:, None]], axis=-1)
    west_part = lax.dynamic_slice_in_dim(west_full, part * part_rows, part_rows + 2, axis=1)
    east_part = lax.dynamic_slice_in_dim(east_full, part * part_rows, part_rows + 2, axis=1)
    above = jnp.where(part == 0, south, halo_block[:, 0, :])
    below = jnp.where(part == parts - 1, north, halo_block[:, -1, :])
    middle = jnp.concatenate([above[:, None, :], block, below[:, None, :]], axis=1)
    extended = jnp.concatenate([west_part[:, :, None], middle, east_part[:, :, None]], axis=2)
    return stencil(extended, block, rate, wet)


def local(forcing, lateral_mix, sea_mask, convective, mixing_inverse, seam_links):
    tracers, depth, rows, cols = forcing.shape
    parts = lax.axis_size("lev")
    part_rows = rows // parts
    part = lax.axis_index("lev")
    codes = seam_links[0] % 4
    wet = sea_mask.astype(jnp.float32)[None]
    plane_rate = jnp.tile(lateral_mix, tracers)[:, None, None]
    wet_rows = lax.dynamic_slice_in_dim(wet, part * part_rows, part_rows, axis=1)
    is_convective = convective == 1
    halo_convective = lax.dynamic_slice_in_dim(
        jnp.pad(is_convective, ((1, 1), (0, 0))), part * part_rows, part_rows + 2, axis=0
    )
    first_map = jnp.concatenate(
        [
            halo_convective.reshape(-1),
            is_convective[:, 0],
            is_convective[:, -1],
            is_convective[0, :],
            is_convective[-1, :],
        ]
    )
    convective_rows = lax.dynamic_slice_in_dim(
        is_convective, part * part_rows, part_rows, axis=0
    ).reshape(-1)
    stacked_inverse = jnp.swapaxes(mixing_inverse, 2, 3).reshape(
        mixing_inverse.shape[0], -1, mixing_inverse.shape[2]
    )
    lateral = horizontal(forcing.reshape(tracers * depth, rows, cols), plane_rate, wet, codes)
    gathered, all_rates = to_rows(lateral.reshape(tracers, depth, rows, cols), lateral_mix)
    block_rate = jnp.tile(all_rates, tracers)[:, None, None]
    mixed = column_mix(gathered, stacked_inverse, first_map)
    levels = mixed.shape[1]
    halo_width = (part_rows + 2) * cols
    halo_block = mixed[:, :, :halo_width].reshape(tracers * levels, part_rows + 2, cols)
    edges = mixed[:, :, halo_width:].reshape(tracers * levels, -1)
    lateral = horizontal_rows(halo_block, edges, block_rate, wet_rows, codes)
    block = column_mix(
        lateral.reshape(tracers, levels, part_rows * cols), stacked_inverse, convective_rows
    )
    return to_levels(block.reshape(tracers, levels, part_rows, cols))


def solution(mesh):
    return jax.shard_map(
        local,
        mesh=mesh,
        in_specs=(
            P(None, "lev", "tile", None),
            P("lev"),
            P("tile", None),
            P("tile", None),
            P(),
            P("tile", None),
        ),
        out_specs=P(None, "lev", "tile", None),
        check_vma=False,
    )
```

```python
import jax
import jax.numpy as jnp
from jax import lax
from jax.sharding import PartitionSpec as P

STEPS = 2
GRID_ROWS = 8

SLOT_STEPS = ((-1, 0), (1, 0), (0, -1), (0, 1), (-1, -1), (-1, 1), (1, -1), (1, 1))


def slot_pairs(count, slot):
    width = count // GRID_ROWS
    row_move, col_move = SLOT_STEPS[slot]
    pairs = []
    for target in range(count):
        row, col = divmod(target, width)
        source = ((row + row_move) % GRID_ROWS) * width + (col + col_move) % width
        pairs.append((source, target))
    return pairs


def pick(pair, code):
    strip = jnp.where(code % 2 == 0, pair[..., 0, :], pair[..., 1, :])
    return jnp.where(code // 2 == 1, strip[..., ::-1], strip)


def stencil(extended, field, rate, wet):
    edge_sum = (
        extended[..., :-2, 1:-1]
        + extended[..., 2:, 1:-1]
        + extended[..., 1:-1, :-2]
        + extended[..., 1:-1, 2:]
    )
    diag_sum = (
        extended[..., :-2, :-2]
        + extended[..., :-2, 2:]
        + extended[..., 2:, :-2]
        + extended[..., 2:, 2:]
    )
    return wet * ((1.0 - 6.0 * rate) * field + rate * edge_sum + 0.5 * rate * diag_sum)


def fetch_seams(strip_pair, corner_set):
    count = lax.axis_size("tile")
    parts = lax.axis_size("lev")
    both = ("tile", "lev")

    def lifted(slot_of_part):
        return [
            (source * parts + lev, target * parts + lev)
            for lev in range(parts)
            for source, target in slot_pairs(count, slot_of_part(lev))
        ]

    got_strips = lax.ppermute(strip_pair, both, lifted(lambda lev: lev))
    got_corners = lax.ppermute(corner_set, both, lifted(lambda lev: 4 + lev))
    return jnp.concatenate([got_strips, got_corners], axis=-1)


def seam_pieces(shared, codes, rows, cols):
    def strips(got, length):
        return jnp.stack([got[..., :length], got[..., length : 2 * length]], axis=-2)

    def corner(slot):
        cell = shared[slot - 4, :, 2 * cols : 2 * cols + 4]
        code = codes[slot]
        return jnp.where(
            code == 0,
            cell[..., 0],
            jnp.where(code == 1, cell[..., 1], jnp.where(code == 2, cell[..., 2], cell[..., 3])),
        )

    south = pick(strips(shared[0], cols), codes[0])
    north = pick(strips(shared[1], cols), codes[1])
    west = pick(strips(shared[2], rows), codes[2])
    east = pick(strips(shared[3], rows), codes[3])
    return south, north, west, east, [corner(slot) for slot in range(4, 8)]


def horizontal(field, rate, wet, codes, tracers):
    parts = lax.axis_size("lev")
    part = lax.axis_index("lev")
    planes, rows, cols = field.shape
    depth = planes // tracers
    own = jnp.concatenate(
        [
            field[:, 0, :],
            field[:, -1, :],
            jnp.pad(jnp.concatenate([field[:, :, 0], field[:, :, -1]], axis=-1), ((0, 0), (0, 2 * (cols - rows)))),
            jnp.stack([field[:, 0, 0], field[:, 0, -1], field[:, -1, 0], field[:, -1, -1]], axis=-1),
        ],
        axis=-1,
    )
    gathered = lax.all_gather(own, "lev")
    every = jnp.transpose(gathered.reshape(parts, tracers, depth, -1), (1, 0, 2, 3)).reshape(
        tracers * parts * depth, -1
    )
    strip_pair = jnp.where(part < 2, every[:, : 2 * cols], every[:, 2 * cols : 4 * cols])
    fetched = fetch_seams(strip_pair, every[:, 4 * cols :])
    outgoing = jnp.transpose(fetched.reshape(tracers, parts, depth, -1), (1, 0, 2, 3))
    shared = lax.all_to_all(outgoing, "lev", 0, 0, tiled=True).reshape(parts, planes, -1)
    south, north, west, east, corners = seam_pieces(shared, codes, rows, cols)
    middle = jnp.concatenate([west[..., None], field, east[..., None]], axis=-1)
    top_row = jnp.concatenate([corners[0][..., None], south, corners[1][..., None]], axis=-1)
    bottom_row = jnp.concatenate([corners[2][..., None], north, corners[3][..., None]], axis=-1)
    extended = jnp.concatenate([top_row[..., None, :], middle, bottom_row[..., None, :]], axis=-2)
    return stencil(extended, field, rate, wet)


def to_rows(lateral, rate):
    parts = lax.axis_size("lev")
    tracers, depth, rows, cols = lateral.shape
    part_rows = rows // parts
    padded = jnp.pad(lateral, ((0, 0), (0, 0), (1, 1), (0, 0)))
    rate_column = jnp.broadcast_to(rate[None, :, None], (tracers, depth, 1))
    edges = jnp.concatenate(
        [lateral[..., :, 0], lateral[..., :, -1], lateral[..., 0, :], lateral[..., -1, :], rate_column],
        axis=-1,
    )
    outgoing = []
    for dest in range(parts):
        window = padded[:, :, dest * part_rows : dest * part_rows + part_rows + 2, :]
        outgoing.append(
            jnp.concatenate([window.reshape(tracers, depth, (part_rows + 2) * cols), edges], axis=-1)
        )
    columns = lax.all_to_all(jnp.stack(outgoing), "lev", 0, 0, tiled=True)
    gathered = jnp.transpose(columns, (1, 0, 2, 3)).reshape(tracers, parts * depth, -1)
    return gathered[..., :-1], gathered[0, :, -1]


def to_levels(block):
    parts = lax.axis_size("lev")
    tracers, levels, part_rows, cols = block.shape
    depth = levels // parts
    outgoing = jnp.transpose(block.reshape(tracers, parts, depth, part_rows, cols), (1, 0, 2, 3, 4))
    returning = lax.all_to_all(outgoing, "lev", 0, 0, tiled=True)
    return jnp.transpose(returning, (1, 2, 0, 3, 4)).reshape(tracers, depth, parts * part_rows, cols)


def column_mix(block, stacked_inverse, convective_map):
    tracers, levels, width = block.shape
    mixed = []
    for tracer in range(tracers):
        both_states = jnp.dot(
            stacked_inverse[tracer], block[tracer], precision=lax.Precision.HIGHEST
        ).reshape(2, levels, width)
        mixed.append(jnp.where(convective_map[None], both_states[1], both_states[0]))
    return jnp.stack(mixed)


def horizontal_rows(halo_block, edges, rate, wet, codes):
    count = lax.axis_size("tile")
    parts = lax.axis_size("lev")
    part = lax.axis_index("lev")
    planes, halo_rows, cols = halo_block.shape
    part_rows = halo_rows - 2
    rows = parts * part_rows
    block = halo_block[:, 1:-1, :]
    first_col = edges[:, :rows]
    last_col = edges[:, rows : 2 * rows]
    first_row = edges[:, 2 * rows : 2 * rows + cols]
    last_row = edges[:, 2 * rows + cols :]
    corner_set = jnp.stack(
        [first_row[:, 0], first_row[:, -1], last_row[:, 0], last_row[:, -1]], axis=-1
    )
    row_pair = jnp.concatenate([first_row, last_row], axis=-1)
    col_pair = jnp.pad(jnp.concatenate([first_col, last_col], axis=-1), ((0, 0), (0, 2 * (cols - rows))))
    fetched = fetch_seams(jnp.where(part < 2, row_pair, col_pair), corner_set)
    shared = lax.all_gather(fetched, "lev")
    south, north, west, east, corners = seam_pieces(shared, codes, rows, cols)
    west_full = jnp.concatenate([corners[0][:, None], west, corners[2][:, None]], axis=-1)
    east_full = jnp.concatenate([corners[1][:, None], east, corners[3][:, None]], axis=-1)
    west_part = lax.dynamic_slice_in_dim(west_full, part * part_rows, part_rows + 2, axis=1)
    east_part = lax.dynamic_slice_in_dim(east_full, part * part_rows, part_rows + 2, axis=1)
    above = jnp.where(part == 0, south, halo_block[:, 0, :])
    below = jnp.where(part == parts - 1, north, halo_block[:, -1, :])
    middle = jnp.concatenate([above[:, None, :], block, below[:, None, :]], axis=1)
    extended = jnp.concatenate([west_part[:, :, None], middle, east_part[:, :, None]], axis=2)
    return stencil(extended, block, rate, wet)


def local(forcing, lateral_mix, sea_mask, convective, mixing_inverse, seam_links):
    tracers, depth, rows, cols = forcing.shape
    parts = lax.axis_size("lev")
    part_rows = rows // parts
    part = lax.axis_index("lev")
    codes = seam_links[0] % 4
    wet = sea_mask.astype(jnp.float32)[None]
    plane_rate = jnp.tile(lateral_mix, tracers)[:, None, None]
    wet_rows = lax.dynamic_slice_in_dim(wet, part * part_rows, part_rows, axis=1)
    is_convective = convective == 1
    halo_convective = lax.dynamic_slice_in_dim(
        jnp.pad(is_convective, ((1, 1), (0, 0))), part * part_rows, part_rows + 2, axis=0
    )
    first_map = jnp.concatenate(
        [
            halo_convective.reshape(-1),
            is_convective[:, 0],
            is_convective[:, -1],
            is_convective[0, :],
            is_convective[-1, :],
        ]
    )
    convective_rows = lax.dynamic_slice_in_dim(
        is_convective, part * part_rows, part_rows, axis=0
    ).reshape(-1)
    stacked_inverse = jnp.swapaxes(mixing_inverse, 2, 3).reshape(
        mixing_inverse.shape[0], -1, mixing_inverse.shape[2]
    )
    lateral = horizontal(forcing.reshape(tracers * depth, rows, cols), plane_rate, wet, codes, tracers)
    gathered, all_rates = to_rows(lateral.reshape(tracers, depth, rows, cols), lateral_mix)
    block_rate = jnp.tile(all_rates, tracers)[:, None, None]
    mixed = column_mix(gathered, stacked_inverse, first_map)
    levels = mixed.shape[1]
    halo_width = (part_rows + 2) * cols
    halo_block = mixed[:, :, :halo_width].reshape(tracers * levels, part_rows + 2, cols)
    edges = mixed[:, :, halo_width:].reshape(tracers * levels, -1)
    lateral = horizontal_rows(halo_block, edges, block_rate, wet_rows, codes)
    block = column_mix(
        lateral.reshape(tracers, levels, part_rows * cols), stacked_inverse, convective_rows
    )
    return to_levels(block.reshape(tracers, levels, part_rows, cols))


def solution(mesh):
    return jax.shard_map(
        local,
        mesh=mesh,
        in_specs=(
            P(None, "lev", "tile", None),
            P("lev"),
            P("tile", None),
            P("tile", None),
            P(),
            P("tile", None),
        ),
        out_specs=P(None, "lev", "tile", None),
        check_vma=False,
    )
```

```python
import jax
import jax.numpy as jnp
from jax import lax
from jax.sharding import PartitionSpec as P

STEPS = 2
GRID_ROWS = 8

SLOT_STEPS = ((-1, 0), (1, 0), (0, -1), (0, 1), (-1, -1), (-1, 1), (1, -1), (1, 1))


def slot_pairs(count, slot):
    width = count // GRID_ROWS
    row_move, col_move = SLOT_STEPS[slot]
    pairs = []
    for target in range(count):
        row, col = divmod(target, width)
        source = ((row + row_move) % GRID_ROWS) * width + (col + col_move) % width
        pairs.append((source, target))
    return pairs


def pick(pair, code):
    strip = jnp.where(code % 2 == 0, pair[..., 0, :], pair[..., 1, :])
    return jnp.where(code // 2 == 1, strip[..., ::-1], strip)


def stencil(extended, field, rate, wet):
    edge_sum = (
        extended[..., :-2, 1:-1]
        + extended[..., 2:, 1:-1]
        + extended[..., 1:-1, :-2]
        + extended[..., 1:-1, 2:]
    )
    diag_sum = (
        extended[..., :-2, :-2]
        + extended[..., :-2, 2:]
        + extended[..., 2:, :-2]
        + extended[..., 2:, 2:]
    )
    return wet * ((1.0 - 6.0 * rate) * field + rate * edge_sum + 0.5 * rate * diag_sum)


def horizontal(field, rate, wet, codes):
    count = lax.axis_size("tile")
    corner_set = jnp.stack(
        [field[..., 0, 0], field[..., 0, -1], field[..., -1, 0], field[..., -1, -1]], axis=-1
    )
    side = jnp.concatenate([field[..., :, 0], field[..., :, -1], corner_set], axis=-1)
    from_west = lax.ppermute(side, "tile", slot_pairs(count, 2))
    from_east = lax.ppermute(side, "tile", slot_pairs(count, 3))
    cols = field.shape[-1]
    rows = field.shape[-2]
    span = 2 * rows
    upright = jnp.concatenate(
        [field[..., 0, :], field[..., -1, :], from_west[..., span:], from_east[..., span:]], axis=-1
    )
    from_south = lax.ppermute(upright, "tile", slot_pairs(count, 0))
    from_north = lax.ppermute(upright, "tile", slot_pairs(count, 1))

    def strips(got, length):
        return jnp.stack([got[..., :length], got[..., length : 2 * length]], axis=-2)

    south = pick(strips(from_south, cols), codes[0])
    north = pick(strips(from_north, cols), codes[1])
    west = pick(strips(from_west, rows), codes[2])
    east = pick(strips(from_east, rows), codes[3])
    base = 2 * cols
    sources = [
        (from_south, base),
        (from_south, base + 4),
        (from_north, base),
        (from_north, base + 4),
    ]
    corners = []
    for slot, (got, first) in zip(range(4, 8), sources):
        code = codes[slot]
        cell = got[..., first : first + 4]
        value = jnp.where(
            code == 0,
            cell[..., 0],
            jnp.where(code == 1, cell[..., 1], jnp.where(code == 2, cell[..., 2], cell[..., 3])),
        )
        corners.append(value)
    middle = jnp.concatenate([west[..., None], field, east[..., None]], axis=-1)
    top_row = jnp.concatenate([corners[0][..., None], south, corners[1][..., None]], axis=-1)
    bottom_row = jnp.concatenate([corners[2][..., None], north, corners[3][..., None]], axis=-1)
    extended = jnp.concatenate([top_row[..., None, :], middle, bottom_row[..., None, :]], axis=-2)
    return stencil(extended, field, rate, wet)


def to_rows(lateral, rate):
    parts = lax.axis_size("lev")
    tracers, depth, rows, cols = lateral.shape
    part_rows = rows // parts
    padded = jnp.pad(lateral, ((0, 0), (0, 0), (1, 1), (0, 0)))
    rate_column = jnp.broadcast_to(rate[None, :, None], (tracers, depth, 1))
    edges = jnp.concatenate(
        [lateral[..., :, 0], lateral[..., :, -1], lateral[..., 0, :], lateral[..., -1, :], rate_column],
        axis=-1,
    )
    outgoing = []
    for dest in range(parts):
        window = padded[:, :, dest * part_rows : dest * part_rows + part_rows + 2, :]
        outgoing.append(
            jnp.concatenate([window.reshape(tracers, depth, (part_rows + 2) * cols), edges], axis=-1)
        )
    columns = lax.all_to_all(jnp.stack(outgoing), "lev", 0, 0, tiled=True)
    gathered = jnp.transpose(columns, (1, 0, 2, 3)).reshape(tracers, parts * depth, -1)
    return gathered[..., :-1], gathered[0, :, -1]


def to_levels(block):
    parts = lax.axis_size("lev")
    tracers, levels, part_rows, cols = block.shape
    depth = levels // parts
    outgoing = jnp.transpose(block.reshape(tracers, parts, depth, part_rows, cols), (1, 0, 2, 3, 4))
    returning = lax.all_to_all(outgoing, "lev", 0, 0, tiled=True)
    return jnp.transpose(returning, (1, 2, 0, 3, 4)).reshape(tracers, depth, parts * part_rows, cols)


def column_mix(block, stacked_inverse, convective_map):
    tracers, levels, width = block.shape
    mixed = []
    for tracer in range(tracers):
        both_states = jnp.dot(
            stacked_inverse[tracer], block[tracer], precision=lax.Precision.HIGHEST
        ).reshape(2, levels, width)
        mixed.append(jnp.where(convective_map[None], both_states[1], both_states[0]))
    return jnp.stack(mixed)


def horizontal_rows(halo_block, edges, rate, wet, codes):
    count = lax.axis_size("tile")
    parts = lax.axis_size("lev")
    part = lax.axis_index("lev")
    planes, halo_rows, cols = halo_block.shape
    part_rows = halo_rows - 2
    rows = parts * part_rows
    block = halo_block[:, 1:-1, :]
    first_col = edges[:, :rows]
    last_col = edges[:, rows : 2 * rows]
    first_row = edges[:, 2 * rows : 2 * rows + cols]
    last_row = edges[:, 2 * rows + cols :]
    corner_set = jnp.stack(
        [first_row[:, 0], first_row[:, -1], last_row[:, 0], last_row[:, -1]], axis=-1
    )
    row_pair = jnp.concatenate([first_row, last_row], axis=-1)
    col_pair = jnp.pad(jnp.concatenate([first_col, last_col], axis=-1), ((0, 0), (0, 2 * (cols - rows))))
    strip_pair = jnp.where(part < 2, row_pair, col_pair)
    both = ("tile", "lev")

    def lifted(slot_of_part):
        return [
            (source * parts + lev, target * parts + lev)
            for lev in range(parts)
            for source, target in slot_pairs(count, slot_of_part(lev))
        ]

    got_strips = lax.ppermute(strip_pair, both, lifted(lambda lev: lev))
    got_corners = lax.ppermute(corner_set, both, lifted(lambda lev: 4 + lev))

    def strips(got, length):
        return jnp.stack([got[..., :length], got[..., length : 2 * length]], axis=-2)

    code = codes[part]
    picked_row = pick(strips(got_strips, cols), code)
    picked_col = jnp.pad(pick(strips(got_strips, rows), code), ((0, 0), (0, cols - rows)))
    corner_code = codes[4 + part]
    picked_corner = jnp.where(
        corner_code == 0,
        got_corners[:, 0],
        jnp.where(
            corner_code == 1,
            got_corners[:, 1],
            jnp.where(corner_code == 2, got_corners[:, 2], got_corners[:, 3]),
        ),
    )
    mine = jnp.concatenate(
        [jnp.where(part < 2, picked_row, picked_col), picked_corner[:, None]], axis=-1
    )
    shared = lax.all_gather(mine, "lev")
    south = shared[0, :, :cols]
    north = shared[1, :, :cols]
    west = shared[2, :, :rows]
    east = shared[3, :, :rows]

    def corner(slot):
        return shared[slot - 4, :, cols]

    west_full = jnp.concatenate([corner(4)[:, None], west, corner(6)[:, None]], axis=-1)
    east_full = jnp.concatenate([corner(5)[:, None], east, corner(7)[:, None]], axis=-1)
    west_part = lax.dynamic_slice_in_dim(west_full, part * part_rows, part_rows + 2, axis=1)
    east_part = lax.dynamic_slice_in_dim(east_full, part * part_rows, part_rows + 2, axis=1)
    above = jnp.where(part == 0, south, halo_block[:, 0, :])
    below = jnp.where(part == parts - 1, north, halo_block[:, -1, :])
    middle = jnp.concatenate([above[:, None, :], block, below[:, None, :]], axis=1)
    extended = jnp.concatenate([west_part[:, :, None], middle, east_part[:, :, None]], axis=2)
    return stencil(extended, block, rate, wet)


def local(forcing, lateral_mix, sea_mask, convective, mixing_inverse, seam_links):
    tracers, depth, rows, cols = forcing.shape
    parts = lax.axis_size("lev")
    part_rows = rows // parts
    part = lax.axis_index("lev")
    codes = seam_links[0] % 4
    wet = sea_mask.astype(jnp.float32)[None]
    plane_rate = jnp.tile(lateral_mix, tracers)[:, None, None]
    wet_rows = lax.dynamic_slice_in_dim(wet, part * part_rows, part_rows, axis=1)
    is_convective = convective == 1
    halo_convective = lax.dynamic_slice_in_dim(
        jnp.pad(is_convective, ((1, 1), (0, 0))), part * part_rows, part_rows + 2, axis=0
    )
    first_map = jnp.concatenate(
        [
            halo_convective.reshape(-1),
            is_convective[:, 0],
            is_convective[:, -1],
            is_convective[0, :],
            is_convective[-1, :],
        ]
    )
    convective_rows = lax.dynamic_slice_in_dim(
        is_convective, part * part_rows, part_rows, axis=0
    ).reshape(-1)
    stacked_inverse = jnp.swapaxes(mixing_inverse, 2, 3).reshape(
        mixing_inverse.shape[0], -1, mixing_inverse.shape[2]
    )
    lateral = horizontal(forcing.reshape(tracers * depth, rows, cols), plane_rate, wet, codes)
    gathered, all_rates = to_rows(lateral.reshape(tracers, depth, rows, cols), lateral_mix)
    block_rate = jnp.tile(all_rates, tracers)[:, None, None]
    mixed = column_mix(gathered, stacked_inverse, first_map)
    levels = mixed.shape[1]
    halo_width = (part_rows + 2) * cols
    halo_block = mixed[:, :, :halo_width].reshape(tracers * levels, part_rows + 2, cols)
    edges = mixed[:, :, halo_width:].reshape(tracers * levels, -1)
    lateral = horizontal_rows(halo_block, edges, block_rate, wet_rows, codes)
    block = column_mix(
        lateral.reshape(tracers, levels, part_rows * cols), stacked_inverse, convective_rows
    )
    return to_levels(block.reshape(tracers, levels, part_rows, cols))


def solution(mesh):
    return jax.shard_map(
        local,
        mesh=mesh,
        in_specs=(
            P(None, "lev", "tile", None),
            P("lev"),
            P("tile", None),
            P("tile", None),
            P(),
            P("tile", None),
        ),
        out_specs=P(None, "lev", "tile", None),
        check_vma=False,
    )
```

```python
import jax
import jax.numpy as jnp
from jax import lax
from jax.sharding import PartitionSpec as P

STEPS = 2
GRID_ROWS = 8

SLOT_STEPS = ((-1, 0), (1, 0), (0, -1), (0, 1), (-1, -1), (-1, 1), (1, -1), (1, 1))


def slot_pairs(count, slot):
    width = count // GRID_ROWS
    row_move, col_move = SLOT_STEPS[slot]
    pairs = []
    for target in range(count):
        row, col = divmod(target, width)
        source = ((row + row_move) % GRID_ROWS) * width + (col + col_move) % width
        pairs.append((source, target))
    return pairs


def pick(pair, code):
    strip = jnp.where(code % 2 == 0, pair[..., 0, :], pair[..., 1, :])
    return jnp.where(code // 2 == 1, strip[..., ::-1], strip)


def stencil(extended, field, rate, wet):
    edge_sum = (
        extended[..., :-2, 1:-1]
        + extended[..., 2:, 1:-1]
        + extended[..., 1:-1, :-2]
        + extended[..., 1:-1, 2:]
    )
    diag_sum = (
        extended[..., :-2, :-2]
        + extended[..., :-2, 2:]
        + extended[..., 2:, :-2]
        + extended[..., 2:, 2:]
    )
    return wet * ((1.0 - 6.0 * rate) * field + rate * edge_sum + 0.5 * rate * diag_sum)


def horizontal(field, rate, wet, codes):
    count = lax.axis_size("tile")
    corner_set = jnp.stack(
        [field[..., 0, 0], field[..., 0, -1], field[..., -1, 0], field[..., -1, -1]], axis=-1
    )
    side = jnp.concatenate([field[..., :, 0], field[..., :, -1], corner_set], axis=-1)
    from_west = lax.ppermute(side, "tile", slot_pairs(count, 2))
    from_east = lax.ppermute(side, "tile", slot_pairs(count, 3))
    cols = field.shape[-1]
    rows = field.shape[-2]
    span = 2 * rows
    upright = jnp.concatenate(
        [field[..., 0, :], field[..., -1, :], from_west[..., span:], from_east[..., span:]], axis=-1
    )
    from_south = lax.ppermute(upright, "tile", slot_pairs(count, 0))
    from_north = lax.ppermute(upright, "tile", slot_pairs(count, 1))

    def strips(got, length):
        return jnp.stack([got[..., :length], got[..., length : 2 * length]], axis=-2)

    south = pick(strips(from_south, cols), codes[0])
    north = pick(strips(from_north, cols), codes[1])
    west = pick(strips(from_west, rows), codes[2])
    east = pick(strips(from_east, rows), codes[3])
    base = 2 * cols
    sources = [
        (from_south, base),
        (from_south, base + 4),
        (from_north, base),
        (from_north, base + 4),
    ]
    corners = []
    for slot, (got, first) in zip(range(4, 8), sources):
        code = codes[slot]
        cell = got[..., first : first + 4]
        value = jnp.where(
            code == 0,
            cell[..., 0],
            jnp.where(code == 1, cell[..., 1], jnp.where(code == 2, cell[..., 2], cell[..., 3])),
        )
        corners.append(value)
    middle = jnp.concatenate([west[..., None], field, east[..., None]], axis=-1)
    top_row = jnp.concatenate([corners[0][..., None], south, corners[1][..., None]], axis=-1)
    bottom_row = jnp.concatenate([corners[2][..., None], north, corners[3][..., None]], axis=-1)
    extended = jnp.concatenate([top_row[..., None, :], middle, bottom_row[..., None, :]], axis=-2)
    return stencil(extended, field, rate, wet)


def to_rows(lateral, rate):
    parts = lax.axis_size("lev")
    tracers, depth, rows, cols = lateral.shape
    part_rows = rows // parts
    padded = jnp.pad(lateral, ((0, 0), (0, 0), (1, 1), (0, 0)))
    rate_column = jnp.broadcast_to(rate[None, :, None], (tracers, depth, 1))
    edges = jnp.concatenate(
        [lateral[..., 0, :], lateral[..., -1, :], lateral[..., :, 0], lateral[..., :, -1], rate_column],
        axis=-1,
    )
    outgoing = []
    for dest in range(parts):
        window = padded[:, :, dest * part_rows : dest * part_rows + part_rows + 2, :]
        outgoing.append(
            jnp.concatenate([window.reshape(tracers, depth, (part_rows + 2) * cols), edges], axis=-1)
        )
    columns = lax.all_to_all(jnp.stack(outgoing), "lev", 0, 0, tiled=True)
    gathered = jnp.transpose(columns, (1, 0, 2, 3)).reshape(tracers, parts * depth, -1)
    return gathered[..., :-1], gathered[0, :, -1]


def to_levels(block):
    parts = lax.axis_size("lev")
    tracers, levels, part_rows, cols = block.shape
    depth = levels // parts
    outgoing = jnp.transpose(block.reshape(tracers, parts, depth, part_rows, cols), (1, 0, 2, 3, 4))
    returning = lax.all_to_all(outgoing, "lev", 0, 0, tiled=True)
    return jnp.transpose(returning, (1, 2, 0, 3, 4)).reshape(tracers, depth, parts * part_rows, cols)


def column_mix(block, stacked_inverse, convective_map):
    tracers, levels, width = block.shape
    mixed = []
    for tracer in range(tracers):
        both_states = jnp.dot(
            stacked_inverse[tracer], block[tracer], precision=lax.Precision.HIGHEST
        ).reshape(2, levels, width)
        mixed.append(jnp.where(convective_map[None], both_states[1], both_states[0]))
    return jnp.stack(mixed)


def horizontal_rows(halo_block, edges, rate, wet, codes):
    count = lax.axis_size("tile")
    parts = lax.axis_size("lev")
    part = lax.axis_index("lev")
    planes, halo_rows, cols = halo_block.shape
    part_rows = halo_rows - 2
    rows = parts * part_rows
    block = halo_block[:, 1:-1, :]
    first_row = edges[:, :cols]
    last_row = edges[:, cols : 2 * cols]
    first_col = edges[:, 2 * cols : 2 * cols + rows]
    last_col = edges[:, 2 * cols + rows :]
    corner_set = jnp.stack(
        [first_row[:, 0], first_row[:, -1], last_row[:, 0], last_row[:, -1]], axis=-1
    )
    row_pair = jnp.concatenate([first_row, last_row], axis=-1)
    col_pair = jnp.pad(jnp.concatenate([first_col, last_col], axis=-1), ((0, 0), (0, 2 * (cols - rows))))
    strip_pair = jnp.where(part < 2, row_pair, col_pair)
    both = ("tile", "lev")

    def lifted(slot_of_part):
        return [
            (source * parts + lev, target * parts + lev)
            for lev in range(parts)
            for source, target in slot_pairs(count, slot_of_part(lev))
        ]

    got_strips = lax.ppermute(strip_pair, both, lifted(lambda lev: lev))
    got_corners = lax.ppermute(corner_set, both, lifted(lambda lev: 4 + lev))
    shared = lax.all_gather(jnp.concatenate([got_strips, got_corners], axis=-1), "lev")

    def strips(got, length):
        return jnp.stack([got[..., :length], got[..., length : 2 * length]], axis=-2)

    def corner(slot):
        cell = shared[slot - 4, :, 2 * cols : 2 * cols + 4]
        code = codes[slot]
        return jnp.where(
            code == 0,
            cell[..., 0],
            jnp.where(code == 1, cell[..., 1], jnp.where(code == 2, cell[..., 2], cell[..., 3])),
        )

    south = pick(strips(shared[0], cols), codes[0])
    north = pick(strips(shared[1], cols), codes[1])
    west = pick(strips(shared[2], rows), codes[2])
    east = pick(strips(shared[3], rows), codes[3])
    west_full = jnp.concatenate([corner(4)[:, None], west, corner(6)[:, None]], axis=-1)
    east_full = jnp.concatenate([corner(5)[:, None], east, corner(7)[:, None]], axis=-1)
    west_part = lax.dynamic_slice_in_dim(west_full, part * part_rows, part_rows + 2, axis=1)
    east_part = lax.dynamic_slice_in_dim(east_full, part * part_rows, part_rows + 2, axis=1)
    above = jnp.where(part == 0, south, halo_block[:, 0, :])
    below = jnp.where(part == parts - 1, north, halo_block[:, -1, :])
    middle = jnp.concatenate([above[:, None, :], block, below[:, None, :]], axis=1)
    extended = jnp.concatenate([west_part[:, :, None], middle, east_part[:, :, None]], axis=2)
    return stencil(extended, block, rate, wet)


def local(forcing, lateral_mix, sea_mask, convective, mixing_inverse, seam_links):
    tracers, depth, rows, cols = forcing.shape
    parts = lax.axis_size("lev")
    part_rows = rows // parts
    part = lax.axis_index("lev")
    codes = seam_links[0] % 4
    wet = sea_mask.astype(jnp.float32)[None]
    plane_rate = jnp.tile(lateral_mix, tracers)[:, None, None]
    wet_rows = lax.dynamic_slice_in_dim(wet, part * part_rows, part_rows, axis=1)
    is_convective = convective == 1
    halo_convective = lax.dynamic_slice_in_dim(
        jnp.pad(is_convective, ((1, 1), (0, 0))), part * part_rows, part_rows + 2, axis=0
    )
    first_map = jnp.concatenate(
        [
            halo_convective.reshape(-1),
            is_convective[0, :],
            is_convective[-1, :],
            is_convective[:, 0],
            is_convective[:, -1],
        ]
    )
    convective_rows = lax.dynamic_slice_in_dim(
        is_convective, part * part_rows, part_rows, axis=0
    ).reshape(-1)
    stacked_inverse = jnp.swapaxes(mixing_inverse, 2, 3).reshape(
        mixing_inverse.shape[0], -1, mixing_inverse.shape[2]
    )
    lateral = horizontal(forcing.reshape(tracers * depth, rows, cols), plane_rate, wet, codes)
    gathered, all_rates = to_rows(lateral.reshape(tracers, depth, rows, cols), lateral_mix)
    block_rate = jnp.tile(all_rates, tracers)[:, None, None]
    mixed = column_mix(gathered, stacked_inverse, first_map)
    levels = mixed.shape[1]
    halo_width = (part_rows + 2) * cols
    halo_block = mixed[:, :, :halo_width].reshape(tracers * levels, part_rows + 2, cols)
    edges = mixed[:, :, halo_width:].reshape(tracers * levels, -1)
    lateral = horizontal_rows(halo_block, edges, block_rate, wet_rows, codes)
    block = column_mix(
        lateral.reshape(tracers, levels, part_rows * cols), stacked_inverse, convective_rows
    )
    return to_levels(block.reshape(tracers, levels, part_rows, cols))


def solution(mesh):
    return jax.shard_map(
        local,
        mesh=mesh,
        in_specs=(
            P(None, "lev", "tile", None),
            P("lev"),
            P("tile", None),
            P("tile", None),
            P(),
            P("tile", None),
        ),
        out_specs=P(None, "lev", "tile", None),
        check_vma=False,
    )
```

```python
import jax
import jax.numpy as jnp
from jax import lax
from jax.sharding import PartitionSpec as P

STEPS = 2
GRID_ROWS = 8

SLOT_STEPS = ((-1, 0), (1, 0), (0, -1), (0, 1), (-1, -1), (-1, 1), (1, -1), (1, 1))


def slot_pairs(count, slot):
    width = count // GRID_ROWS
    row_move, col_move = SLOT_STEPS[slot]
    pairs = []
    for target in range(count):
        row, col = divmod(target, width)
        source = ((row + row_move) % GRID_ROWS) * width + (col + col_move) % width
        pairs.append((source, target))
    return pairs


def pick(pair, code):
    strip = jnp.where(code % 2 == 0, pair[..., 0, :], pair[..., 1, :])
    return jnp.where(code // 2 == 1, strip[..., ::-1], strip)


def stencil(extended, field, rate, wet):
    edge_sum = (
        extended[..., :-2, 1:-1]
        + extended[..., 2:, 1:-1]
        + extended[..., 1:-1, :-2]
        + extended[..., 1:-1, 2:]
    )
    diag_sum = (
        extended[..., :-2, :-2]
        + extended[..., :-2, 2:]
        + extended[..., 2:, :-2]
        + extended[..., 2:, 2:]
    )
    return wet * ((1.0 - 6.0 * rate) * field + rate * edge_sum + 0.5 * rate * diag_sum)


def horizontal(field, rate, wet, codes):
    count = lax.axis_size("tile")
    corner_set = jnp.stack(
        [field[..., 0, 0], field[..., 0, -1], field[..., -1, 0], field[..., -1, -1]], axis=-1
    )
    side = jnp.concatenate([field[..., :, 0], field[..., :, -1], corner_set], axis=-1)
    from_west = lax.ppermute(side, "tile", slot_pairs(count, 2))
    from_east = lax.ppermute(side, "tile", slot_pairs(count, 3))
    cols = field.shape[-1]
    rows = field.shape[-2]
    span = 2 * rows
    upright = jnp.concatenate(
        [field[..., 0, :], field[..., -1, :], from_west[..., span:], from_east[..., span:]], axis=-1
    )
    from_south = lax.ppermute(upright, "tile", slot_pairs(count, 0))
    from_north = lax.ppermute(upright, "tile", slot_pairs(count, 1))

    def strips(got, length):
        return jnp.stack([got[..., :length], got[..., length : 2 * length]], axis=-2)

    south = pick(strips(from_south, cols), codes[0])
    north = pick(strips(from_north, cols), codes[1])
    west = pick(strips(from_west, rows), codes[2])
    east = pick(strips(from_east, rows), codes[3])
    base = 2 * cols
    sources = [
        (from_south, base),
        (from_south, base + 4),
        (from_north, base),
        (from_north, base + 4),
    ]
    corners = []
    for slot, (got, first) in zip(range(4, 8), sources):
        code = codes[slot]
        cell = got[..., first : first + 4]
        value = jnp.where(
            code == 0,
            cell[..., 0],
            jnp.where(code == 1, cell[..., 1], jnp.where(code == 2, cell[..., 2], cell[..., 3])),
        )
        corners.append(value)
    middle = jnp.concatenate([west[..., None], field, east[..., None]], axis=-1)
    top_row = jnp.concatenate([corners[0][..., None], south, corners[1][..., None]], axis=-1)
    bottom_row = jnp.concatenate([corners[2][..., None], north, corners[3][..., None]], axis=-1)
    extended = jnp.concatenate([top_row[..., None, :], middle, bottom_row[..., None, :]], axis=-2)
    return stencil(extended, field, rate, wet)


def to_rows(lateral, rate):
    parts = lax.axis_size("lev")
    tracers, depth, rows, cols = lateral.shape
    part_rows = rows // parts
    padded = jnp.pad(lateral, ((0, 0), (0, 0), (1, 1), (0, 0)))
    rate_column = jnp.broadcast_to(rate[None, :, None], (tracers, depth, 1))
    edges = jnp.concatenate(
        [lateral[..., 0, :], lateral[..., -1, :], lateral[..., :, 0], lateral[..., :, -1], rate_column],
        axis=-1,
    )
    outgoing = []
    for dest in range(parts):
        window = padded[:, :, dest * part_rows : dest * part_rows + part_rows + 2, :]
        outgoing.append(
            jnp.concatenate([window.reshape(tracers, depth, (part_rows + 2) * cols), edges], axis=-1)
        )
    columns = lax.all_to_all(jnp.stack(outgoing), "lev", 0, 0, tiled=True)
    gathered = jnp.transpose(columns, (1, 0, 2, 3)).reshape(tracers, parts * depth, -1)
    return gathered[..., :-1], gathered[0, :, -1]


def to_levels(block):
    parts = lax.axis_size("lev")
    tracers, levels, part_rows, cols = block.shape
    depth = levels // parts
    outgoing = jnp.transpose(block.reshape(tracers, parts, depth, part_rows, cols), (1, 0, 2, 3, 4))
    returning = lax.all_to_all(outgoing, "lev", 0, 0, tiled=True)
    return jnp.transpose(returning, (1, 2, 0, 3, 4)).reshape(tracers, depth, parts * part_rows, cols)


def column_mix(block, stacked_inverse, convective_map):
    tracers, levels, width = block.shape
    mixed = []
    for tracer in range(tracers):
        both_states = jnp.dot(
            stacked_inverse[tracer], block[tracer], precision=lax.Precision.HIGHEST
        ).reshape(2, levels, width)
        mixed.append(jnp.where(convective_map[None], both_states[1], both_states[0]))
    return jnp.stack(mixed)


def horizontal_rows(halo_block, edges, rate, wet, codes):
    count = lax.axis_size("tile")
    parts = lax.axis_size("lev")
    part = lax.axis_index("lev")
    planes, halo_rows, cols = halo_block.shape
    part_rows = halo_rows - 2
    rows = parts * part_rows
    block = halo_block[:, 1:-1, :]
    first_row = edges[:, :cols]
    last_row = edges[:, cols : 2 * cols]
    first_col = edges[:, 2 * cols : 2 * cols + rows]
    last_col = edges[:, 2 * cols + rows :]
    corner_set = jnp.stack(
        [first_row[:, 0], first_row[:, -1], last_row[:, 0], last_row[:, -1]], axis=-1
    )
    both = ("tile", "lev")

    def lifted(slot_of_part):
        return [
            (source * parts + lev, target * parts + lev)
            for lev in range(parts)
            for source, target in slot_pairs(count, slot_of_part(lev))
        ]

    col_pair = jnp.concatenate([first_col, last_col], axis=-1)
    row_pair = jnp.concatenate([first_row, last_row], axis=-1)
    last = parts - 1
    from_west = lax.ppermute(col_pair, both, lifted(lambda lev: 2))
    from_east = lax.ppermute(col_pair, both, lifted(lambda lev: 3))
    from_row = lax.ppermute(row_pair, both, lifted(lambda lev: 1 if lev == last else 0))
    first_corner = lax.ppermute(corner_set, both, lifted(lambda lev: 6 if lev == last else 4))
    second_corner = lax.ppermute(corner_set, both, lifted(lambda lev: 7 if lev == last else 5))

    def strips(got, length):
        return jnp.stack([got[..., :length], got[..., length : 2 * length]], axis=-2)

    def choose(cell, code):
        return jnp.where(
            code == 0,
            cell[..., 0],
            jnp.where(code == 1, cell[..., 1], jnp.where(code == 2, cell[..., 2], cell[..., 3])),
        )

    at_end = part == last
    row_code = jnp.where(at_end, codes[1], codes[0])
    outer = pick(strips(from_row, cols), row_code)
    south = outer
    north = outer
    west = pick(strips(from_west, rows), codes[2])
    east = pick(strips(from_east, rows), codes[3])
    corner_a = choose(first_corner, jnp.where(at_end, codes[6], codes[4]))
    corner_b = choose(second_corner, jnp.where(at_end, codes[7], codes[5]))
    west_full = jnp.concatenate([corner_a[:, None], west, corner_a[:, None]], axis=-1)
    east_full = jnp.concatenate([corner_b[:, None], east, corner_b[:, None]], axis=-1)
    west_part = lax.dynamic_slice_in_dim(west_full, part * part_rows, part_rows + 2, axis=1)
    east_part = lax.dynamic_slice_in_dim(east_full, part * part_rows, part_rows + 2, axis=1)
    above = jnp.where(part == 0, south, halo_block[:, 0, :])
    below = jnp.where(part == parts - 1, north, halo_block[:, -1, :])
    middle = jnp.concatenate([above[:, None, :], block, below[:, None, :]], axis=1)
    extended = jnp.concatenate([west_part[:, :, None], middle, east_part[:, :, None]], axis=2)
    return stencil(extended, block, rate, wet)


def local(forcing, lateral_mix, sea_mask, convective, mixing_inverse, seam_links):
    tracers, depth, rows, cols = forcing.shape
    parts = lax.axis_size("lev")
    part_rows = rows // parts
    part = lax.axis_index("lev")
    codes = seam_links[0] % 4
    wet = sea_mask.astype(jnp.float32)[None]
    plane_rate = jnp.tile(lateral_mix, tracers)[:, None, None]
    wet_rows = lax.dynamic_slice_in_dim(wet, part * part_rows, part_rows, axis=1)
    is_convective = convective == 1
    halo_convective = lax.dynamic_slice_in_dim(
        jnp.pad(is_convective, ((1, 1), (0, 0))), part * part_rows, part_rows + 2, axis=0
    )
    first_map = jnp.concatenate(
        [
            halo_convective.reshape(-1),
            is_convective[0, :],
            is_convective[-1, :],
            is_convective[:, 0],
            is_convective[:, -1],
        ]
    )
    convective_rows = lax.dynamic_slice_in_dim(
        is_convective, part * part_rows, part_rows, axis=0
    ).reshape(-1)
    stacked_inverse = jnp.swapaxes(mixing_inverse, 2, 3).reshape(
        mixing_inverse.shape[0], -1, mixing_inverse.shape[2]
    )
    lateral = horizontal(forcing.reshape(tracers * depth, rows, cols), plane_rate, wet, codes)
    gathered, all_rates = to_rows(lateral.reshape(tracers, depth, rows, cols), lateral_mix)
    block_rate = jnp.tile(all_rates, tracers)[:, None, None]
    mixed = column_mix(gathered, stacked_inverse, first_map)
    levels = mixed.shape[1]
    halo_width = (part_rows + 2) * cols
    halo_block = mixed[:, :, :halo_width].reshape(tracers * levels, part_rows + 2, cols)
    edges = mixed[:, :, halo_width:].reshape(tracers * levels, -1)
    lateral = horizontal_rows(halo_block, edges, block_rate, wet_rows, codes)
    block = column_mix(
        lateral.reshape(tracers, levels, part_rows * cols), stacked_inverse, convective_rows
    )
    return to_levels(block.reshape(tracers, levels, part_rows, cols))


def solution(mesh):
    return jax.shard_map(
        local,
        mesh=mesh,
        in_specs=(
            P(None, "lev", "tile", None),
            P("lev"),
            P("tile", None),
            P("tile", None),
            P(),
            P("tile", None),
        ),
        out_specs=P(None, "lev", "tile", None),
        check_vma=False,
    )
```

```python
import jax
import jax.numpy as jnp
from jax import lax
from jax.sharding import PartitionSpec as P

STEPS = 2
GRID_ROWS = 8

SLOT_STEPS = ((-1, 0), (1, 0), (0, -1), (0, 1), (-1, -1), (-1, 1), (1, -1), (1, 1))


def slot_pairs(count, slot):
    width = count // GRID_ROWS
    row_move, col_move = SLOT_STEPS[slot]
    pairs = []
    for target in range(count):
        row, col = divmod(target, width)
        source = ((row + row_move) % GRID_ROWS) * width + (col + col_move) % width
        pairs.append((source, target))
    return pairs


def pick(pair, code):
    strip = jnp.where(code % 2 == 0, pair[..., 0, :], pair[..., 1, :])
    return jnp.where(code // 2 == 1, strip[..., ::-1], strip)


def stencil(extended, field, rate, wet):
    edge_sum = (
        extended[..., :-2, 1:-1]
        + extended[..., 2:, 1:-1]
        + extended[..., 1:-1, :-2]
        + extended[..., 1:-1, 2:]
    )
    diag_sum = (
        extended[..., :-2, :-2]
        + extended[..., :-2, 2:]
        + extended[..., 2:, :-2]
        + extended[..., 2:, 2:]
    )
    return wet * ((1.0 - 6.0 * rate) * field + rate * edge_sum + 0.5 * rate * diag_sum)


def horizontal(field, rate, wet, codes):
    count = lax.axis_size("tile")
    corner_set = jnp.stack(
        [field[..., 0, 0], field[..., 0, -1], field[..., -1, 0], field[..., -1, -1]], axis=-1
    )
    side = jnp.concatenate([field[..., :, 0], field[..., :, -1], corner_set], axis=-1)
    from_west = lax.ppermute(side, "tile", slot_pairs(count, 2))
    from_east = lax.ppermute(side, "tile", slot_pairs(count, 3))
    cols = field.shape[-1]
    rows = field.shape[-2]
    span = 2 * rows
    upright = jnp.concatenate(
        [field[..., 0, :], field[..., -1, :], from_west[..., span:], from_east[..., span:]], axis=-1
    )
    from_south = lax.ppermute(upright, "tile", slot_pairs(count, 0))
    from_north = lax.ppermute(upright, "tile", slot_pairs(count, 1))

    def strips(got, length):
        return jnp.stack([got[..., :length], got[..., length : 2 * length]], axis=-2)

    south = pick(strips(from_south, cols), codes[0])
    north = pick(strips(from_north, cols), codes[1])
    west = pick(strips(from_west, rows), codes[2])
    east = pick(strips(from_east, rows), codes[3])
    base = 2 * cols
    sources = [
        (from_south, base),
        (from_south, base + 4),
        (from_north, base),
        (from_north, base + 4),
    ]
    corners = []
    for slot, (got, first) in zip(range(4, 8), sources):
        code = codes[slot]
        cell = got[..., first : first + 4]
        value = jnp.where(
            code == 0,
            cell[..., 0],
            jnp.where(code == 1, cell[..., 1], jnp.where(code == 2, cell[..., 2], cell[..., 3])),
        )
        corners.append(value)
    middle = jnp.concatenate([west[..., None], field, east[..., None]], axis=-1)
    top_row = jnp.concatenate([corners[0][..., None], south, corners[1][..., None]], axis=-1)
    bottom_row = jnp.concatenate([corners[2][..., None], north, corners[3][..., None]], axis=-1)
    extended = jnp.concatenate([top_row[..., None, :], middle, bottom_row[..., None, :]], axis=-2)
    return stencil(extended, field, rate, wet)


def to_rows(lateral, rate):
    parts = lax.axis_size("lev")
    tracers, depth, rows, cols = lateral.shape
    part_rows = rows // parts
    padded = jnp.pad(lateral, ((0, 0), (0, 0), (1, 1), (0, 0)))
    rate_column = jnp.broadcast_to(rate[None, :, None], (tracers, depth, 1))
    row_edges = jnp.concatenate([lateral[..., 0, :], lateral[..., -1, :], rate_column], axis=-1)
    col_edges = jnp.concatenate(
        [
            lateral[..., :, 0],
            lateral[..., :, -1],
            jnp.zeros((tracers, depth, 2 * (cols - rows)), lateral.dtype),
            rate_column,
        ],
        axis=-1,
    )
    outgoing = []
    for dest in range(parts):
        window = padded[:, :, dest * part_rows : dest * part_rows + part_rows + 2, :]
        edges = row_edges if dest < 2 else col_edges
        outgoing.append(
            jnp.concatenate([window.reshape(tracers, depth, (part_rows + 2) * cols), edges], axis=-1)
        )
    columns = lax.all_to_all(jnp.stack(outgoing), "lev", 0, 0, tiled=True)
    gathered = jnp.transpose(columns, (1, 0, 2, 3)).reshape(tracers, parts * depth, -1)
    return gathered[..., :-1], gathered[0, :, -1]


def to_levels(block):
    parts = lax.axis_size("lev")
    tracers, levels, part_rows, cols = block.shape
    depth = levels // parts
    outgoing = jnp.transpose(block.reshape(tracers, parts, depth, part_rows, cols), (1, 0, 2, 3, 4))
    returning = lax.all_to_all(outgoing, "lev", 0, 0, tiled=True)
    return jnp.transpose(returning, (1, 2, 0, 3, 4)).reshape(tracers, depth, parts * part_rows, cols)


def column_mix(block, stacked_inverse, convective_map):
    tracers, levels, width = block.shape
    mixed = []
    for tracer in range(tracers):
        both_states = jnp.dot(
            stacked_inverse[tracer], block[tracer], precision=lax.Precision.HIGHEST
        ).reshape(2, levels, width)
        mixed.append(jnp.where(convective_map[None], both_states[1], both_states[0]))
    return jnp.stack(mixed)


def horizontal_rows(halo_block, edges, rate, wet, codes):
    count = lax.axis_size("tile")
    parts = lax.axis_size("lev")
    part = lax.axis_index("lev")
    planes, halo_rows, cols = halo_block.shape
    part_rows = halo_rows - 2
    rows = parts * part_rows
    block = halo_block[:, 1:-1, :]
    from_rows = jnp.stack([edges[:, 0], edges[:, cols - 1], edges[:, cols], edges[:, 2 * cols - 1]], axis=-1)
    from_cols = jnp.stack(
        [edges[:, 0], edges[:, rows], edges[:, rows - 1], edges[:, 2 * rows - 1]], axis=-1
    )
    corner_set = jnp.where(part < 2, from_rows, from_cols)
    strip_pair = edges
    both = ("tile", "lev")

    def lifted(slot_of_part):
        return [
            (source * parts + lev, target * parts + lev)
            for lev in range(parts)
            for source, target in slot_pairs(count, slot_of_part(lev))
        ]

    got_strips = lax.ppermute(strip_pair, both, lifted(lambda lev: lev))
    got_corners = lax.ppermute(corner_set, both, lifted(lambda lev: 4 + lev))
    shared = lax.all_gather(jnp.concatenate([got_strips, got_corners], axis=-1), "lev")

    def strips(got, length):
        return jnp.stack([got[..., :length], got[..., length : 2 * length]], axis=-2)

    def corner(slot):
        cell = shared[slot - 4, :, 2 * cols : 2 * cols + 4]
        code = codes[slot]
        return jnp.where(
            code == 0,
            cell[..., 0],
            jnp.where(code == 1, cell[..., 1], jnp.where(code == 2, cell[..., 2], cell[..., 3])),
        )

    south = pick(strips(shared[0], cols), codes[0])
    north = pick(strips(shared[1], cols), codes[1])
    west = pick(strips(shared[2], rows), codes[2])
    east = pick(strips(shared[3], rows), codes[3])
    west_full = jnp.concatenate([corner(4)[:, None], west, corner(6)[:, None]], axis=-1)
    east_full = jnp.concatenate([corner(5)[:, None], east, corner(7)[:, None]], axis=-1)
    west_part = lax.dynamic_slice_in_dim(west_full, part * part_rows, part_rows + 2, axis=1)
    east_part = lax.dynamic_slice_in_dim(east_full, part * part_rows, part_rows + 2, axis=1)
    above = jnp.where(part == 0, south, halo_block[:, 0, :])
    below = jnp.where(part == parts - 1, north, halo_block[:, -1, :])
    middle = jnp.concatenate([above[:, None, :], block, below[:, None, :]], axis=1)
    extended = jnp.concatenate([west_part[:, :, None], middle, east_part[:, :, None]], axis=2)
    return stencil(extended, block, rate, wet)


def local(forcing, lateral_mix, sea_mask, convective, mixing_inverse, seam_links):
    tracers, depth, rows, cols = forcing.shape
    parts = lax.axis_size("lev")
    part_rows = rows // parts
    part = lax.axis_index("lev")
    codes = seam_links[0] % 4
    wet = sea_mask.astype(jnp.float32)[None]
    plane_rate = jnp.tile(lateral_mix, tracers)[:, None, None]
    wet_rows = lax.dynamic_slice_in_dim(wet, part * part_rows, part_rows, axis=1)
    is_convective = convective == 1
    halo_convective = lax.dynamic_slice_in_dim(
        jnp.pad(is_convective, ((1, 1), (0, 0))), part * part_rows, part_rows + 2, axis=0
    )
    row_map = jnp.concatenate([is_convective[0, :], is_convective[-1, :]])
    col_map = jnp.concatenate(
        [is_convective[:, 0], is_convective[:, -1], jnp.zeros((2 * (cols - rows),), bool)]
    )
    first_map = jnp.concatenate(
        [halo_convective.reshape(-1), jnp.where(part < 2, row_map, col_map)]
    )
    convective_rows = lax.dynamic_slice_in_dim(
        is_convective, part * part_rows, part_rows, axis=0
    ).reshape(-1)
    stacked_inverse = jnp.swapaxes(mixing_inverse, 2, 3).reshape(
        mixing_inverse.shape[0], -1, mixing_inverse.shape[2]
    )
    lateral = horizontal(forcing.reshape(tracers * depth, rows, cols), plane_rate, wet, codes)
    gathered, all_rates = to_rows(lateral.reshape(tracers, depth, rows, cols), lateral_mix)
    block_rate = jnp.tile(all_rates, tracers)[:, None, None]
    mixed = column_mix(gathered, stacked_inverse, first_map)
    levels = mixed.shape[1]
    halo_width = (part_rows + 2) * cols
    halo_block = mixed[:, :, :halo_width].reshape(tracers * levels, part_rows + 2, cols)
    edges = mixed[:, :, halo_width:].reshape(tracers * levels, -1)
    lateral = horizontal_rows(halo_block, edges, block_rate, wet_rows, codes)
    block = column_mix(
        lateral.reshape(tracers, levels, part_rows * cols), stacked_inverse, convective_rows
    )
    return to_levels(block.reshape(tracers, levels, part_rows, cols))


def solution(mesh):
    return jax.shard_map(
        local,
        mesh=mesh,
        in_specs=(
            P(None, "lev", "tile", None),
            P("lev"),
            P("tile", None),
            P("tile", None),
            P(),
            P("tile", None),
        ),
        out_specs=P(None, "lev", "tile", None),
        check_vma=False,
    )
```

```python
import jax
import jax.numpy as jnp
from jax import lax
from jax.sharding import PartitionSpec as P

STEPS = 2
GRID_ROWS = 8

SLOT_STEPS = ((-1, 0), (1, 0), (0, -1), (0, 1), (-1, -1), (-1, 1), (1, -1), (1, 1))


def slot_pairs(count, slot):
    width = count // GRID_ROWS
    row_move, col_move = SLOT_STEPS[slot]
    pairs = []
    for target in range(count):
        row, col = divmod(target, width)
        source = ((row + row_move) % GRID_ROWS) * width + (col + col_move) % width
        pairs.append((source, target))
    return pairs


def pick(pair, code):
    strip = jnp.where(code % 2 == 0, pair[..., 0, :], pair[..., 1, :])
    return jnp.where(code // 2 == 1, strip[..., ::-1], strip)


def stencil(extended, field, rate, wet):
    edge_sum = (
        extended[..., :-2, 1:-1]
        + extended[..., 2:, 1:-1]
        + extended[..., 1:-1, :-2]
        + extended[..., 1:-1, 2:]
    )
    diag_sum = (
        extended[..., :-2, :-2]
        + extended[..., :-2, 2:]
        + extended[..., 2:, :-2]
        + extended[..., 2:, 2:]
    )
    return wet * ((1.0 - 6.0 * rate) * field + rate * edge_sum + 0.5 * rate * diag_sum)


def horizontal(field, rate, wet, codes):
    count = lax.axis_size("tile")
    corner_set = jnp.stack(
        [field[..., 0, 0], field[..., 0, -1], field[..., -1, 0], field[..., -1, -1]], axis=-1
    )
    side = jnp.concatenate([field[..., :, 0], field[..., :, -1], corner_set], axis=-1)
    from_west = lax.ppermute(side, "tile", slot_pairs(count, 2))
    from_east = lax.ppermute(side, "tile", slot_pairs(count, 3))
    cols = field.shape[-1]
    rows = field.shape[-2]
    span = 2 * rows
    upright = jnp.concatenate(
        [field[..., 0, :], field[..., -1, :], from_west[..., span:], from_east[..., span:]], axis=-1
    )
    from_south = lax.ppermute(upright, "tile", slot_pairs(count, 0))
    from_north = lax.ppermute(upright, "tile", slot_pairs(count, 1))

    def strips(got, length):
        return jnp.stack([got[..., :length], got[..., length : 2 * length]], axis=-2)

    south = pick(strips(from_south, cols), codes[0])
    north = pick(strips(from_north, cols), codes[1])
    west = pick(strips(from_west, rows), codes[2])
    east = pick(strips(from_east, rows), codes[3])
    base = 2 * cols
    sources = [
        (from_south, base),
        (from_south, base + 4),
        (from_north, base),
        (from_north, base + 4),
    ]
    corners = []
    for slot, (got, first) in zip(range(4, 8), sources):
        code = codes[slot]
        cell = got[..., first : first + 4]
        value = jnp.where(
            code == 0,
            cell[..., 0],
            jnp.where(code == 1, cell[..., 1], jnp.where(code == 2, cell[..., 2], cell[..., 3])),
        )
        corners.append(value)
    middle = jnp.concatenate([west[..., None], field, east[..., None]], axis=-1)
    top_row = jnp.concatenate([corners[0][..., None], south, corners[1][..., None]], axis=-1)
    bottom_row = jnp.concatenate([corners[2][..., None], north, corners[3][..., None]], axis=-1)
    extended = jnp.concatenate([top_row[..., None, :], middle, bottom_row[..., None, :]], axis=-2)
    return stencil(extended, field, rate, wet)


def to_rows(lateral, rate):
    parts = lax.axis_size("lev")
    tracers, depth, rows, cols = lateral.shape
    part_rows = rows // parts
    padded = jnp.pad(lateral, ((0, 0), (0, 0), (1, 1), (0, 0)))
    rate_column = jnp.broadcast_to(rate[None, :, None], (tracers, depth, 1))
    edges = jnp.concatenate(
        [lateral[..., 0, :], lateral[..., -1, :], lateral[..., :, 0], lateral[..., :, -1], rate_column],
        axis=-1,
    )
    outgoing = []
    for dest in range(parts):
        window = padded[:, :, dest * part_rows : dest * part_rows + part_rows + 2, :]
        outgoing.append(
            jnp.concatenate([window.reshape(tracers, depth, (part_rows + 2) * cols), edges], axis=-1)
        )
    columns = lax.all_to_all(jnp.stack(outgoing), "lev", 0, 0, tiled=True)
    gathered = jnp.transpose(columns, (1, 0, 2, 3)).reshape(tracers, parts * depth, -1)
    return gathered[..., :-1], gathered[0, :, -1]


def to_levels(outgoing, rows, cols):
    parts, tracers, depth, width = outgoing.shape
    returning = lax.all_to_all(outgoing, "lev", 0, 0, tiled=True)
    return jnp.transpose(returning, (1, 2, 0, 3)).reshape(tracers, depth, rows, cols)


def column_mix(block, stacked_inverse, convective_map):
    tracers, levels, width = block.shape
    mixed = []
    for tracer in range(tracers):
        both_states = jnp.dot(
            stacked_inverse[tracer], block[tracer], precision=lax.Precision.HIGHEST
        ).reshape(2, levels, width)
        mixed.append(jnp.where(convective_map[None], both_states[1], both_states[0]))
    return jnp.stack(mixed)


def horizontal_rows(halo_block, edges, rate, wet, codes):
    count = lax.axis_size("tile")
    parts = lax.axis_size("lev")
    part = lax.axis_index("lev")
    planes, halo_rows, cols = halo_block.shape
    part_rows = halo_rows - 2
    rows = parts * part_rows
    block = halo_block[:, 1:-1, :]
    first_row = edges[:, :cols]
    last_row = edges[:, cols : 2 * cols]
    first_col = edges[:, 2 * cols : 2 * cols + rows]
    last_col = edges[:, 2 * cols + rows :]
    corner_set = jnp.stack(
        [first_row[:, 0], first_row[:, -1], last_row[:, 0], last_row[:, -1]], axis=-1
    )
    row_pair = jnp.concatenate([first_row, last_row], axis=-1)
    col_pair = jnp.pad(jnp.concatenate([first_col, last_col], axis=-1), ((0, 0), (0, 2 * (cols - rows))))
    strip_pair = jnp.where(part < 2, row_pair, col_pair)
    both = ("tile", "lev")

    def lifted(slot_of_part):
        return [
            (source * parts + lev, target * parts + lev)
            for lev in range(parts)
            for source, target in slot_pairs(count, slot_of_part(lev))
        ]

    got_strips = lax.ppermute(strip_pair, both, lifted(lambda lev: lev))
    got_corners = lax.ppermute(corner_set, both, lifted(lambda lev: 4 + lev))
    shared = lax.all_gather(jnp.concatenate([got_strips, got_corners], axis=-1), "lev")

    def strips(got, length):
        return jnp.stack([got[..., :length], got[..., length : 2 * length]], axis=-2)

    def corner(slot):
        cell = shared[slot - 4, :, 2 * cols : 2 * cols + 4]
        code = codes[slot]
        return jnp.where(
            code == 0,
            cell[..., 0],
            jnp.where(code == 1, cell[..., 1], jnp.where(code == 2, cell[..., 2], cell[..., 3])),
        )

    south = pick(strips(shared[0], cols), codes[0])
    north = pick(strips(shared[1], cols), codes[1])
    west = pick(strips(shared[2], rows), codes[2])
    east = pick(strips(shared[3], rows), codes[3])
    west_full = jnp.concatenate([corner(4)[:, None], west, corner(6)[:, None]], axis=-1)
    east_full = jnp.concatenate([corner(5)[:, None], east, corner(7)[:, None]], axis=-1)
    west_part = lax.dynamic_slice_in_dim(west_full, part * part_rows, part_rows + 2, axis=1)
    east_part = lax.dynamic_slice_in_dim(east_full, part * part_rows, part_rows + 2, axis=1)
    above = jnp.where(part == 0, south, halo_block[:, 0, :])
    below = jnp.where(part == parts - 1, north, halo_block[:, -1, :])
    middle = jnp.concatenate([above[:, None, :], block, below[:, None, :]], axis=1)
    extended = jnp.concatenate([west_part[:, :, None], middle, east_part[:, :, None]], axis=2)
    return stencil(extended, block, rate, wet)


def local(forcing, lateral_mix, sea_mask, convective, mixing_inverse, seam_links):
    tracers, depth, rows, cols = forcing.shape
    parts = lax.axis_size("lev")
    part_rows = rows // parts
    part = lax.axis_index("lev")
    codes = seam_links[0] % 4
    wet = sea_mask.astype(jnp.float32)[None]
    plane_rate = jnp.tile(lateral_mix, tracers)[:, None, None]
    wet_rows = lax.dynamic_slice_in_dim(wet, part * part_rows, part_rows, axis=1)
    is_convective = convective == 1
    halo_convective = lax.dynamic_slice_in_dim(
        jnp.pad(is_convective, ((1, 1), (0, 0))), part * part_rows, part_rows + 2, axis=0
    )
    first_map = jnp.concatenate(
        [
            halo_convective.reshape(-1),
            is_convective[0, :],
            is_convective[-1, :],
            is_convective[:, 0],
            is_convective[:, -1],
        ]
    )
    convective_rows = lax.dynamic_slice_in_dim(
        is_convective, part * part_rows, part_rows, axis=0
    ).reshape(-1)
    stacked_inverse = jnp.swapaxes(mixing_inverse, 2, 3).reshape(
        mixing_inverse.shape[0], -1, mixing_inverse.shape[2]
    )
    lateral = horizontal(forcing.reshape(tracers * depth, rows, cols), plane_rate, wet, codes)
    gathered, all_rates = to_rows(lateral.reshape(tracers, depth, rows, cols), lateral_mix)
    block_rate = jnp.tile(all_rates, tracers)[:, None, None]
    mixed = column_mix(gathered, stacked_inverse, first_map)
    levels = mixed.shape[1]
    halo_width = (part_rows + 2) * cols
    halo_block = mixed[:, :, :halo_width].reshape(tracers * levels, part_rows + 2, cols)
    edges = mixed[:, :, halo_width:].reshape(tracers * levels, -1)
    lateral = horizontal_rows(halo_block, edges, block_rate, wet_rows, codes)
    flat = lateral.reshape(tracers, levels, part_rows * cols)
    outgoing = []
    for tracer in range(tracers):
        both_states = jnp.dot(
            stacked_inverse[tracer], flat[tracer], precision=lax.Precision.HIGHEST
        ).reshape(2, parts, depth, part_rows * cols)
        outgoing.append(jnp.where(convective_rows[None, None], both_states[1], both_states[0]))
    return to_levels(jnp.stack(outgoing, axis=1), rows, cols)


def solution(mesh):
    return jax.shard_map(
        local,
        mesh=mesh,
        in_specs=(
            P(None, "lev", "tile", None),
            P("lev"),
            P("tile", None),
            P("tile", None),
            P(),
            P("tile", None),
        ),
        out_specs=P(None, "lev", "tile", None),
        check_vma=False,
    )
```
